128 devices in a mesh: sta: 32 (over y, x, z_hi), tm: 4 (over z_lo, core).
Axes of the slice: x: 4, y: 4, z: 4 (z_hi: 2, z_lo: 2; z = z_hi * 2 + z_lo), core: 2. Of those that a mesh axis runs over, the one named last changes fastest.
Arguments:
- spectra: bfloat16 [8, 4096, 2, 4096], P('tm', None, None, 'sta')
- src_ids: int32 [3, 8], replicated, may hold values from 0 to 4095, as said below
Outputs:
- correlations: float32 [3, 256, 8, 4096], P(None, 'tm', None, 'sta')
The draws below stay inside these ranges and needn't reach their ends.
Inputs may be any that keep to these rules, and one draw needn't show every extreme that they name: `src_ids`: the 8 ids of a round are distinct and all lie in one block of 128 consecutive stations that starts at a multiple of 128.
All inputs are finite; a program needn't handle non-finite values.
Results may differ from the reference program's by a relative error of at most 0.0056.
Values may be sent and summed in bfloat16 or wider, within the bound.
No kernel may reach another device: no remote copies, remote signals or barrier semaphores. Data moves between devices by JAX's collectives and lax.ppermute only.
A program may use at most 128 MiB of HBM per device.

```python
import math
import jax
import jax.numpy as jnp
from jax import lax

STA_DEV = 128
HR_DEV = 2
BINS = 4096
BLOCK = 64
LAGS = 256
NSRC = 8
ROUNDS = 3
STATIONS = 4096
HOURS = 8


def draw_spectra(key, part):
    key_base, key_row, key_block = jax.random.split(jax.random.fold_in(key, 11), 3)
    block_num = BINS // BLOCK
    full = (HOURS, STATIONS, 2, block_num, BLOCK)
    base = jnp.clip(jax.random.normal(key_base, full, jnp.float32), -6.0, 6.0)
    row_scale = jnp.exp(jax.random.uniform(key_row, (HOURS, STATIONS, 1, 1, 1), jnp.float32, 0.0, math.log(10.0)))
    block_scale = jnp.exp(jax.random.uniform(key_block, (HOURS, STATIONS, 1, block_num, 1), jnp.float32, 0.0, math.log(10.0)))
    return (base * row_scale * block_scale).reshape(HOURS, STATIONS, 2, BINS).astype(jnp.bfloat16)


def draw_src_ids(key, part):
    key_owner, key_order, key_shift, key_shuffle = jax.random.split(jax.random.fold_in(key, 23), 4)
    shard_count = STATIONS // STA_DEV
    owners = jax.random.randint(key_owner, (ROUNDS,), 0, shard_count)
    chosen = jax.random.permutation(key_order, ROUNDS)
    owners = owners.at[chosen[0]].set(0).at[chosen[1]].set(shard_count - 1)
    shifts = jax.random.randint(key_shift, (ROUNDS,), 0, STA_DEV)
    shifts = shifts.at[chosen[0]].set(0).at[chosen[1]].set(STA_DEV - 1)
    shuffles = jax.vmap(lambda one_key: jax.random.permutation(one_key, STA_DEV))(jax.random.split(key_shuffle, ROUNDS))
    offsets = jnp.remainder(shuffles - shuffles[:, :1] + shifts[:, None], STA_DEV)
    return (owners[:, None] * STA_DEV + offsets[:, :NSRC]).astype(jnp.int32)


def setup_inputs(seed: int = 0) -> dict:
    key_of = jax.random.split(jax.random.key(seed), 3)
    spectra = draw_spectra(jax.random.fold_in(key_of[2], 71), 0)
    src_ids = draw_src_ids(jax.random.fold_in(key_of[2], 71), 0)
    return dict(spectra=spectra, src_ids=src_ids)


EPSILON = 1e-05

def block_sums(spec):
    values = spec.astype(jnp.float32)
    magnitude = jnp.sqrt(values[..., 0, :] * values[..., 0, :] + values[..., 1, :] * values[..., 1, :])
    full_shape = magnitude.shape
    return magnitude.reshape(full_shape[:-1] + (full_shape[-1] // BLOCK, BLOCK)).sum(axis=-1)

def level_divide(spec, padded):
    block_num = padded.shape[-1] - 2
    level_mean = (padded[..., :-2] + padded[..., 1:-1] + padded[..., 2:]) / (3.0 * BLOCK)
    full_shape = spec.shape
    grid_view = spec.astype(jnp.float32).reshape(full_shape[:-1] + (block_num, BLOCK))
    whitened = grid_view / (level_mean[..., None, :, None] + EPSILON)
    return whitened.reshape(full_shape).astype(jnp.bfloat16)

def make_table(total_hours):
    lag_index = lax.iota(jnp.int32, LAGS) - LAGS // 2
    freq_index = lax.iota(jnp.int32, BINS)
    phase_int = jnp.remainder(lag_index[:, None] * freq_index[None, :], 2 * BINS)
    angle_rad = 2.0 * math.pi / (2 * BINS) * phase_int.astype(jnp.float32)
    norm_scale = 1.0 / math.sqrt(BINS * total_hours)
    return jnp.concatenate([jnp.cos(angle_rad) * norm_scale, -jnp.sin(angle_rad) * norm_scale], axis=1).astype(jnp.bfloat16)

def cross_block(sources, receivers):
    source_f = sources.astype(jnp.float32)
    receive_f = receivers.astype(jnp.float32)
    real_part = lax.optimization_barrier(jnp.sum(source_f[:, :, None, 0] * receive_f[:, None, :, 0] + source_f[:, :, None, 1] * receive_f[:, None, :, 1], axis=0))
    imag_part = lax.optimization_barrier(jnp.sum(source_f[:, :, None, 1] * receive_f[:, None, :, 0] - source_f[:, :, None, 0] * receive_f[:, None, :, 1], axis=0))
    count_src = sources.shape[1]
    count_rcv = receivers.shape[1]
    stacked = jnp.stack([real_part, imag_part], axis=2).astype(jnp.bfloat16)
    return stacked.reshape(count_src * count_rcv, 2 * sources.shape[-1])

def reference(spectra, src_ids):

    def whiten_hour(one_hour):
        totals = block_sums(one_hour)
        return level_divide(one_hour, jnp.pad(totals, ((0, 0), (1, 1))))
    whitened = lax.map(whiten_hour, spectra)
    transform = make_table(HOURS).astype(jnp.float32)
    group_count = HOURS // HR_DEV
    block_count = STATIONS // STA_DEV
    results = []
    for step_no in range(ROUNDS):
        sources = jnp.take(whitened, src_ids[step_no], axis=1)

        def one_block(position):
            receivers = lax.dynamic_slice_in_dim(whitened, position * STA_DEV, STA_DEV, 1)
            summed = jnp.zeros((LAGS, NSRC * STA_DEV), jnp.float32)
            for group_no in range(group_count):
                low = group_no * HR_DEV
                cross_spec = cross_block(sources[low:low + HR_DEV], receivers[low:low + HR_DEV])
                summed = summed + lax.dot_general(transform, cross_spec.astype(jnp.float32), (((1,), (1,)), ((), ())), precision=lax.Precision.HIGHEST)
            return summed.reshape(LAGS, NSRC, STA_DEV)
        stacked = lax.map(one_block, jnp.arange(block_count, dtype=jnp.int32))
        results.append(jnp.transpose(stacked, (1, 2, 0, 3)).reshape(LAGS, NSRC, STATIONS))
    return jnp.stack(results)
```

```python
import math

import jax
import jax.numpy as jnp
from jax import lax
from jax.sharding import PartitionSpec as P

BINS = 4096
BLOCK = 64
LAGS = 256
NSRC = 8
ROUNDS = 3


EPSILON = 1e-05


def spread(value, axis, root):
    mine = lax.axis_index(axis) == root
    return lax.psum(jnp.where(mine, value, jnp.zeros_like(value)), axis)


def block_sums(spec):
    values = spec.astype(jnp.float32)
    magnitude = jnp.sqrt(
        values[..., 0, :] * values[..., 0, :] + values[..., 1, :] * values[..., 1, :]
    )
    full_shape = magnitude.shape
    return magnitude.reshape(full_shape[:-1] + (full_shape[-1] // BLOCK, BLOCK)).sum(axis=-1)


def level_divide(spec, padded):
    block_num = padded.shape[-1] - 2
    level_mean = (padded[..., :-2] + padded[..., 1:-1] + padded[..., 2:]) / (3.0 * BLOCK)
    full_shape = spec.shape
    grid_view = spec.astype(jnp.float32).reshape(full_shape[:-1] + (block_num, BLOCK))
    whitened = grid_view / (level_mean[..., None, :, None] + EPSILON)
    return whitened.reshape(full_shape).astype(jnp.bfloat16)


def make_table(total_hours):
    lag_index = lax.iota(jnp.int32, LAGS) - LAGS // 2
    freq_index = lax.iota(jnp.int32, BINS)
    phase_int = jnp.remainder(lag_index[:, None] * freq_index[None, :], 2 * BINS)
    angle_rad = 2.0 * math.pi / (2 * BINS) * phase_int.astype(jnp.float32)
    norm_scale = 1.0 / math.sqrt(BINS * total_hours)
    return jnp.concatenate(
        [jnp.cos(angle_rad) * norm_scale, -jnp.sin(angle_rad) * norm_scale], axis=1
    ).astype(jnp.bfloat16)


def cross_block(sources, receivers):
    source_f = sources.astype(jnp.float32)
    receive_f = receivers.astype(jnp.float32)
    real_part = jnp.sum(
        source_f[:, :, None, 0] * receive_f[:, None, :, 0]
        + source_f[:, :, None, 1] * receive_f[:, None, :, 1],
        axis=0,
    )
    imag_part = jnp.sum(
        source_f[:, :, None, 1] * receive_f[:, None, :, 0]
        - source_f[:, :, None, 0] * receive_f[:, None, :, 1],
        axis=0,
    )
    count_src = sources.shape[1]
    count_rcv = receivers.shape[1]
    stacked = jnp.stack([real_part, imag_part], axis=2).astype(jnp.bfloat16)
    return stacked.reshape(count_src * count_rcv, 2 * sources.shape[-1])


def local(spectra, src_ids):
    flat_ids = src_ids.reshape(-1)
    src_raw = jnp.take(spectra, flat_ids, axis=1)
    src_all = lax.all_gather(src_raw, "sta", axis=3, tiled=True)
    arrived = lax.all_to_all(spectra, "sta", split_axis=1, concat_axis=3, tiled=True)
    totals = block_sums(arrived)
    by_station = level_divide(arrived, jnp.pad(totals, ((0, 0), (0, 0), (1, 1))))
    src_totals = block_sums(src_all)
    src_white = level_divide(src_all, jnp.pad(src_totals, ((0, 0), (0, 0), (1, 1))))
    hours_dev = by_station.shape[0]
    stations_dev = by_station.shape[1]
    transform = make_table(hours_dev * lax.axis_size("tm"))
    row_count = transform.shape[0] // lax.axis_size("tm")
    results = []
    for step_no in range(ROUNDS):
        sources = src_white[:, step_no * NSRC:(step_no + 1) * NSRC]
        cross_spec = cross_block(sources, by_station)
        projected = lax.dot_general(
            transform, cross_spec, (((1,), (1,)), ((), ())), preferred_element_type=jnp.float32
        )
        stacked = lax.psum_scatter(projected, "tm", scatter_dimension=0, tiled=True)
        results.append(stacked.reshape(row_count, NSRC, stations_dev))
    return jnp.stack(results)


def solution(mesh):
    return jax.shard_map(
        local,
        mesh=mesh,
        in_specs=(P("tm", None, None, "sta"), P()),
        out_specs=P(None, "tm", None, "sta"),
        check_vma=False,
    )
```

```python
import math

import jax
import jax.numpy as jnp
from jax import lax
from jax.experimental import pallas as pl
from jax.experimental.pallas import tpu as pltpu
from jax.sharding import PartitionSpec as P

BINS = 4096
BLOCK = 64
LAGS = 256
NSRC = 8
ROUNDS = 3

CHUNK = 256
ROWS = 16

EPSILON = 1e-05


def block_sums(spec):
    values = spec.astype(jnp.float32)
    magnitude = jnp.sqrt(
        values[..., 0, :] * values[..., 0, :] + values[..., 1, :] * values[..., 1, :]
    )
    full_shape = magnitude.shape
    return magnitude.reshape(full_shape[:-1] + (full_shape[-1] // BLOCK, BLOCK)).sum(axis=-1)


def level_divide(spec, padded):
    block_num = padded.shape[-1] - 2
    level_mean = (padded[..., :-2] + padded[..., 1:-1] + padded[..., 2:]) / (3.0 * BLOCK)
    full_shape = spec.shape
    grid_view = spec.astype(jnp.float32).reshape(full_shape[:-1] + (block_num, BLOCK))
    whitened = grid_view / (level_mean[..., None, :, None] + EPSILON)
    return whitened.reshape(full_shape).astype(jnp.bfloat16)


def make_table(total_hours):
    lag_index = lax.iota(jnp.int32, LAGS) - LAGS // 2
    freq_index = lax.iota(jnp.int32, BINS)
    phase_int = jnp.remainder(lag_index[:, None] * freq_index[None, :], 2 * BINS)
    angle_rad = 2.0 * math.pi / (2 * BINS) * phase_int.astype(jnp.float32)
    norm_scale = 1.0 / math.sqrt(BINS * total_hours)
    return jnp.concatenate(
        [jnp.cos(angle_rad) * norm_scale, -jnp.sin(angle_rad) * norm_scale], axis=1
    ).astype(jnp.bfloat16)


def cross_project_kernel(x_ref, y_ref, tre_ref, tim_ref, out_ref, yb_ref, cre_ref, cim_ref):
    step = pl.program_id(0)
    hours = x_ref.shape[0]
    stations = x_ref.shape[2]
    count_src = y_ref.shape[2]
    width = x_ref.shape[3]

    @pl.when(step == 0)
    def _():
        out_ref[...] = jnp.zeros_like(out_ref)

    for h in range(hours):
        for p in range(2):
            for k in range(count_src):
                row = y_ref[h, p, pl.ds(k, 1), :].astype(jnp.float32)
                yb_ref[h, p, k] = jnp.broadcast_to(row, (ROWS, width))

    def body(r, carry):
        first = pl.multiple_of(r * ROWS, ROWS)
        xs = [
            [x_ref[h, p, pl.ds(first, ROWS), :].astype(jnp.float32) for p in range(2)]
            for h in range(hours)
        ]
        for k in range(count_src):
            real = None
            imag = None
            for h in range(hours):
                y0 = yb_ref[h, 0, k]
                y1 = yb_ref[h, 1, k]
                x0, x1 = xs[h]
                re_h = y0 * x0 + y1 * x1
                im_h = y1 * x0 - y0 * x1
                real = re_h if real is None else real + re_h
                imag = im_h if imag is None else imag + im_h
            dest = pl.ds(k * stations + first, ROWS)
            cre_ref[dest, :] = real.astype(jnp.bfloat16)
            cim_ref[dest, :] = imag.astype(jnp.bfloat16)
        return carry

    lax.fori_loop(0, stations // ROWS, body, 0)
    dims = (((1,), (1,)), ((), ()))
    out_ref[...] += lax.dot_general(
        tre_ref[...], cre_ref[...], dims, preferred_element_type=jnp.float32
    ) + lax.dot_general(tim_ref[...], cim_ref[...], dims, preferred_element_type=jnp.float32)


def cross_project(receivers, sources, transform):
    hours, _, stations, bins = receivers.shape
    count_src = sources.shape[2]
    lags = transform.shape[0]
    steps = bins // CHUNK
    return pl.pallas_call(
        cross_project_kernel,
        grid=(steps,),
        in_specs=[
            pl.BlockSpec((hours, 2, stations, CHUNK), lambda j: (0, 0, 0, j)),
            pl.BlockSpec((hours, 2, count_src, CHUNK), lambda j: (0, 0, 0, j)),
            pl.BlockSpec((lags, CHUNK), lambda j: (0, j)),
            pl.BlockSpec((lags, CHUNK), lambda j: (0, j + steps)),
        ],
        out_specs=pl.BlockSpec((lags, count_src * stations), lambda j: (0, 0)),
        out_shape=jax.ShapeDtypeStruct((lags, count_src * stations), jnp.float32),
        scratch_shapes=[
            pltpu.VMEM((hours, 2, count_src, ROWS, CHUNK), jnp.float32),
            pltpu.VMEM((count_src * stations, CHUNK), jnp.bfloat16),
            pltpu.VMEM((count_src * stations, CHUNK), jnp.bfloat16),
        ],
        compiler_params=pltpu.CompilerParams(dimension_semantics=("arbitrary",)),
    )(receivers, sources, transform, transform)


def local(spectra, src_ids):
    flat_ids = src_ids.reshape(-1)
    src_raw = jnp.take(spectra, flat_ids, axis=1)
    src_all = lax.all_gather(src_raw, "sta", axis=3, tiled=True)
    arrived = lax.all_to_all(spectra, "sta", split_axis=1, concat_axis=3, tiled=True)
    stations_dev = arrived.shape[1]
    joined = jnp.concatenate([arrived, src_all], axis=1)
    totals = block_sums(joined)
    white = level_divide(joined, jnp.pad(totals, ((0, 0), (0, 0), (1, 1))))
    white = jnp.transpose(white, (0, 2, 1, 3))
    by_station = white[:, :, :stations_dev]
    src_white = white[:, :, stations_dev:]
    hours_dev = by_station.shape[0]
    transform = make_table(hours_dev * lax.axis_size("tm"))
    row_count = transform.shape[0] // lax.axis_size("tm")
    results = []
    for step_no in range(ROUNDS):
        sources = src_white[:, :, step_no * NSRC:(step_no + 1) * NSRC]
        projected = cross_project(by_station, sources, transform)
        stacked = lax.psum_scatter(projected, "tm", scatter_dimension=0, tiled=True)
        results.append(stacked.reshape(row_count, NSRC, stations_dev))
    return jnp.stack(results)


def solution(mesh):
    return jax.shard_map(
        local,
        mesh=mesh,
        in_specs=(P("tm", None, None, "sta"), P()),
        out_specs=P(None, "tm", None, "sta"),
        check_vma=False,
    )
```

```python
import math

import jax
import jax.numpy as jnp
from jax import lax
from jax.experimental import pallas as pl
from jax.experimental.pallas import tpu as pltpu
from jax.sharding import PartitionSpec as P

BINS = 4096
BLOCK = 64
LAGS = 256
NSRC = 8
ROUNDS = 3

CHUNK = 256
ROWS = 16

EPSILON = 1e-05


def block_sums(spec):
    values = spec.astype(jnp.float32)
    magnitude = jnp.sqrt(
        values[..., 0, :] * values[..., 0, :] + values[..., 1, :] * values[..., 1, :]
    )
    full_shape = magnitude.shape
    return magnitude.reshape(full_shape[:-1] + (full_shape[-1] // BLOCK, BLOCK)).sum(axis=-1)


def level_divide(spec, padded):
    block_num = padded.shape[-1] - 2
    level_mean = (padded[..., :-2] + padded[..., 1:-1] + padded[..., 2:]) / (3.0 * BLOCK)
    full_shape = spec.shape
    grid_view = spec.astype(jnp.float32).reshape(full_shape[:-1] + (block_num, BLOCK))
    whitened = grid_view / (level_mean[..., None, :, None] + EPSILON)
    return whitened.reshape(full_shape).astype(jnp.bfloat16)


def make_table(total_hours):
    lag_index = lax.iota(jnp.int32, LAGS) - LAGS // 2
    freq_index = lax.iota(jnp.int32, BINS)
    phase_int = jnp.remainder(lag_index[:, None] * freq_index[None, :], 2 * BINS)
    angle_rad = 2.0 * math.pi / (2 * BINS) * phase_int.astype(jnp.float32)
    norm_scale = 1.0 / math.sqrt(BINS * total_hours)
    return jnp.concatenate(
        [jnp.cos(angle_rad) * norm_scale, -jnp.sin(angle_rad) * norm_scale], axis=1
    ).astype(jnp.bfloat16)


def cross_project_kernel(x_ref, y_ref, tre_ref, tim_ref, out_ref, yb_ref, cre_ref, cim_ref):
    step = pl.program_id(0)
    hours = x_ref.shape[0]
    stations = x_ref.shape[2]
    count_src = y_ref.shape[2]
    width = x_ref.shape[3]

    @pl.when(step == 0)
    def _():
        out_ref[...] = jnp.zeros_like(out_ref)

    for h in range(hours):
        for p in range(2):
            for k in range(count_src):
                row = y_ref[h, p, pl.ds(k, 1), :].astype(jnp.float32)
                yb_ref[h, p, k] = jnp.broadcast_to(row, (ROWS, width))

    def body(r, carry):
        first = pl.multiple_of(r * ROWS, ROWS)
        xs = [
            [x_ref[h, p, pl.ds(first, ROWS), :].astype(jnp.float32) for p in range(2)]
            for h in range(hours)
        ]
        for k in range(count_src):
            real = None
            imag = None
            for h in range(hours):
                y0 = yb_ref[h, 0, k]
                y1 = yb_ref[h, 1, k]
                x0, x1 = xs[h]
                re_h = y0 * x0 + y1 * x1
                im_h = y1 * x0 - y0 * x1
                real = re_h if real is None else real + re_h
                imag = im_h if imag is None else imag + im_h
            dest = pl.ds(k * stations + first, ROWS)
            cre_ref[dest, :] = real.astype(jnp.bfloat16)
            cim_ref[dest, :] = imag.astype(jnp.bfloat16)
        return carry

    lax.fori_loop(0, stations // ROWS, body, 0)
    dims = (((1,), (1,)), ((), ()))
    out_ref[...] += lax.dot_general(
        tre_ref[...], cre_ref[...], dims, preferred_element_type=jnp.float32
    ) + lax.dot_general(tim_ref[...], cim_ref[...], dims, preferred_element_type=jnp.float32)


def cross_project(receivers, sources, transform, stations):
    hours, _, _, bins = receivers.shape
    count_src = sources.shape[2]
    lags = transform.shape[0]
    steps = bins // CHUNK
    return pl.pallas_call(
        cross_project_kernel,
        grid=(steps,),
        in_specs=[
            pl.BlockSpec((hours, 2, stations, CHUNK), lambda j: (0, 0, 0, j)),
            pl.BlockSpec((hours, 2, count_src, CHUNK), lambda j: (0, 0, 0, j)),
            pl.BlockSpec((lags, CHUNK), lambda j: (0, j)),
            pl.BlockSpec((lags, CHUNK), lambda j: (0, j + steps)),
        ],
        out_specs=pl.BlockSpec((lags, count_src * stations), lambda j: (0, 0)),
        out_shape=jax.ShapeDtypeStruct((lags, count_src * stations), jnp.float32),
        scratch_shapes=[
            pltpu.VMEM((hours, 2, count_src, ROWS, CHUNK), jnp.float32),
            pltpu.VMEM((count_src * stations, CHUNK), jnp.bfloat16),
            pltpu.VMEM((count_src * stations, CHUNK), jnp.bfloat16),
        ],
        compiler_params=pltpu.CompilerParams(dimension_semantics=("arbitrary",)),
    )(receivers, sources, transform, transform)


def local(spectra, src_ids):
    hours_dev, stations, _, bins_dev = spectra.shape
    shards = lax.axis_size("sta")
    stations_dev = stations // shards
    flat_ids = src_ids.reshape(-1)
    count_all = flat_ids.shape[0]
    by_part = jnp.transpose(spectra, (0, 2, 1, 3))
    src_raw = jnp.take(by_part, flat_ids, axis=2)
    chunks = by_part.reshape(hours_dev, 2, shards, stations_dev, bins_dev)
    src_copies = jnp.broadcast_to(
        src_raw[:, :, None], (hours_dev, 2, shards, count_all, bins_dev)
    )
    send = jnp.concatenate([chunks, src_copies], axis=3).reshape(
        hours_dev, 2, shards * (stations_dev + count_all), bins_dev
    )
    joined = lax.all_to_all(send, "sta", split_axis=2, concat_axis=3, tiled=True)
    values = joined.astype(jnp.float32)
    magnitude = jnp.sqrt(values[:, 0] * values[:, 0] + values[:, 1] * values[:, 1])
    rows = magnitude.shape[1]
    block_num = BINS // BLOCK
    totals = magnitude.reshape(hours_dev, rows, block_num, BLOCK).sum(axis=-1)
    padded = jnp.pad(totals, ((0, 0), (0, 0), (1, 1)))
    level_mean = (padded[..., :-2] + padded[..., 1:-1] + padded[..., 2:]) / (3.0 * BLOCK)
    grid_view = values.reshape(hours_dev, 2, rows, block_num, BLOCK)
    white = (grid_view / (level_mean[:, None, :, :, None] + EPSILON)).reshape(values.shape)
    white = white.astype(jnp.bfloat16)
    transform = make_table(hours_dev * lax.axis_size("tm"))
    row_count = transform.shape[0] // lax.axis_size("tm")
    results = []
    for step_no in range(ROUNDS):
        first = stations_dev + step_no * NSRC
        sources = white[:, :, first:first + NSRC]
        projected = cross_project(white, sources, transform, stations_dev)
        stacked = lax.psum_scatter(projected, "tm", scatter_dimension=0, tiled=True)
        results.append(stacked.reshape(row_count, NSRC, stations_dev))
    return jnp.stack(results)


def solution(mesh):
    return jax.shard_map(
        local,
        mesh=mesh,
        in_specs=(P("tm", None, None, "sta"), P()),
        out_specs=P(None, "tm", None, "sta"),
        check_vma=False,
    )
```

```python
import math

import jax
import jax.numpy as jnp
from jax import lax
from jax.experimental import pallas as pl
from jax.experimental.pallas import tpu as pltpu
from jax.sharding import PartitionSpec as P

BINS = 4096
BLOCK = 64
LAGS = 256
NSRC = 8
ROUNDS = 3

CHUNK = 256
ROWS = 16

EPSILON = 1e-05


def block_sums(spec):
    values = spec.astype(jnp.float32)
    magnitude = jnp.sqrt(
        values[..., 0, :] * values[..., 0, :] + values[..., 1, :] * values[..., 1, :]
    )
    full_shape = magnitude.shape
    return magnitude.reshape(full_shape[:-1] + (full_shape[-1] // BLOCK, BLOCK)).sum(axis=-1)


def level_divide(spec, padded):
    block_num = padded.shape[-1] - 2
    level_mean = (padded[..., :-2] + padded[..., 1:-1] + padded[..., 2:]) / (3.0 * BLOCK)
    full_shape = spec.shape
    grid_view = spec.astype(jnp.float32).reshape(full_shape[:-1] + (block_num, BLOCK))
    whitened = grid_view / (level_mean[..., None, :, None] + EPSILON)
    return whitened.reshape(full_shape).astype(jnp.bfloat16)


def make_table(total_hours):
    lag_index = lax.iota(jnp.int32, LAGS) - LAGS // 2
    freq_index = lax.iota(jnp.int32, BINS)
    phase_int = jnp.remainder(lag_index[:, None] * freq_index[None, :], 2 * BINS)
    angle_rad = 2.0 * math.pi / (2 * BINS) * phase_int.astype(jnp.float32)
    norm_scale = 1.0 / math.sqrt(BINS * total_hours)
    return jnp.concatenate(
        [jnp.cos(angle_rad) * norm_scale, -jnp.sin(angle_rad) * norm_scale], axis=1
    ).astype(jnp.bfloat16)


def cross_project_kernel(x_ref, y_ref, tre_ref, tim_ref, out_ref, yb_ref, cre_ref, cim_ref):
    step = pl.program_id(0)
    hours = x_ref.shape[0]
    stations = x_ref.shape[2]
    count_src = y_ref.shape[2]
    width = x_ref.shape[3]

    @pl.when(step == 0)
    def _():
        out_ref[...] = jnp.zeros_like(out_ref)

    for h in range(hours):
        for p in range(2):
            for k in range(count_src):
                row = y_ref[h, p, pl.ds(k, 1), :].astype(jnp.float32)
                yb_ref[h, p, k] = jnp.broadcast_to(row, (ROWS, width))

    def body(r, carry):
        first = pl.multiple_of(r * ROWS, ROWS)
        xs = [
            [x_ref[h, p, pl.ds(first, ROWS), :].astype(jnp.float32) for p in range(2)]
            for h in range(hours)
        ]
        for k in range(count_src):
            real = None
            imag = None
            for h in range(hours):
                y0 = yb_ref[h, 0, k]
                y1 = yb_ref[h, 1, k]
                x0, x1 = xs[h]
                re_h = y0 * x0 + y1 * x1
                im_h = y1 * x0 - y0 * x1
                real = re_h if real is None else real + re_h
                imag = im_h if imag is None else imag + im_h
            dest = pl.ds(k * stations + first, ROWS)
            cre_ref[dest, :] = real.astype(jnp.bfloat16)
            cim_ref[dest, :] = imag.astype(jnp.bfloat16)
        return carry

    lax.fori_loop(0, stations // ROWS, body, 0)
    dims = (((1,), (1,)), ((), ()))
    out_ref[...] += lax.dot_general(
        tre_ref[...], cre_ref[...], dims, preferred_element_type=jnp.float32
    ) + lax.dot_general(tim_ref[...], cim_ref[...], dims, preferred_element_type=jnp.float32)


def cross_project(receivers, sources, transform, stations):
    hours, _, _, bins = receivers.shape
    count_src = sources.shape[2]
    lags = transform.shape[0]
    steps = bins // CHUNK
    return pl.pallas_call(
        cross_project_kernel,
        grid=(steps,),
        in_specs=[
            pl.BlockSpec((hours, 2, stations, CHUNK), lambda j: (0, 0, 0, j)),
            pl.BlockSpec((hours, 2, count_src, CHUNK), lambda j: (0, 0, 0, j)),
            pl.BlockSpec((lags, CHUNK), lambda j: (0, j)),
            pl.BlockSpec((lags, CHUNK), lambda j: (0, j + steps)),
        ],
        out_specs=pl.BlockSpec((lags, count_src * stations), lambda j: (0, 0)),
        out_shape=jax.ShapeDtypeStruct((lags, count_src * stations), jnp.float32),
        scratch_shapes=[
            pltpu.VMEM((hours, 2, count_src, ROWS, CHUNK), jnp.float32),
            pltpu.VMEM((count_src * stations, CHUNK), jnp.bfloat16),
            pltpu.VMEM((count_src * stations, CHUNK), jnp.bfloat16),
        ],
        compiler_params=pltpu.CompilerParams(dimension_semantics=("arbitrary",)),
    )(receivers, sources, transform, transform)


def local(spectra, src_ids):
    hours_dev, stations, _, bins_dev = spectra.shape
    shards = lax.axis_size("sta")
    stations_dev = stations // shards
    flat_ids = src_ids.reshape(-1)
    count_all = flat_ids.shape[0]
    by_part = jnp.transpose(spectra, (0, 2, 1, 3))
    src_raw = jnp.take(by_part, flat_ids, axis=2)
    chunks = by_part.reshape(hours_dev, 2, shards, stations_dev, bins_dev)
    src_copies = jnp.broadcast_to(
        src_raw[:, :, None], (hours_dev, 2, shards, count_all, bins_dev)
    )
    send = jnp.concatenate([chunks, src_copies], axis=3).reshape(
        hours_dev, 2, shards * (stations_dev + count_all), bins_dev
    )
    joined = lax.all_to_all(send, "sta", split_axis=2, concat_axis=3, tiled=True)
    values = joined.astype(jnp.float32)
    magnitude = jnp.sqrt(values[:, 0] * values[:, 0] + values[:, 1] * values[:, 1])
    block_num = BINS // BLOCK
    indicator = (
        lax.broadcasted_iota(jnp.int32, (BINS, block_num), 0) // BLOCK
        == lax.broadcasted_iota(jnp.int32, (BINS, block_num), 1)
    ).astype(jnp.float32)
    totals = jnp.einsum(
        "hrf,fb->hrb", magnitude, indicator, precision=lax.Precision.HIGHEST
    )
    padded = jnp.pad(totals, ((0, 0), (0, 0), (1, 1)))
    level_mean = (padded[..., :-2] + padded[..., 1:-1] + padded[..., 2:]) / (3.0 * BLOCK)
    denom = jnp.einsum(
        "hrb,fb->hrf", level_mean + EPSILON, indicator, precision=lax.Precision.HIGHEST
    )
    white = (values / denom[:, None]).astype(jnp.bfloat16)
    transform = make_table(hours_dev * lax.axis_size("tm"))
    row_count = transform.shape[0] // lax.axis_size("tm")
    results = []
    for step_no in range(ROUNDS):
        first = stations_dev + step_no * NSRC
        sources = white[:, :, first:first + NSRC]
        projected = cross_project(white, sources, transform, stations_dev)
        stacked = lax.psum_scatter(projected, "tm", scatter_dimension=0, tiled=True)
        results.append(stacked.reshape(row_count, NSRC, stations_dev))
    return jnp.stack(results)


def solution(mesh):
    return jax.shard_map(
        local,
        mesh=mesh,
        in_specs=(P("tm", None, None, "sta"), P()),
        out_specs=P(None, "tm", None, "sta"),
        check_vma=False,
    )
```

```python
import math

import jax
import jax.numpy as jnp
from jax import lax
from jax.experimental import pallas as pl
from jax.experimental.pallas import tpu as pltpu
from jax.sharding import PartitionSpec as P

BINS = 4096
BLOCK = 64
LAGS = 256
NSRC = 8
ROUNDS = 3

CHUNK = 256
ROWS = 16

EPSILON = 1e-05


def block_sums(spec):
    values = spec.astype(jnp.float32)
    magnitude = jnp.sqrt(
        values[..., 0, :] * values[..., 0, :] + values[..., 1, :] * values[..., 1, :]
    )
    full_shape = magnitude.shape
    return magnitude.reshape(full_shape[:-1] + (full_shape[-1] // BLOCK, BLOCK)).sum(axis=-1)


def level_divide(spec, padded):
    block_num = padded.shape[-1] - 2
    level_mean = (padded[..., :-2] + padded[..., 1:-1] + padded[..., 2:]) / (3.0 * BLOCK)
    full_shape = spec.shape
    grid_view = spec.astype(jnp.float32).reshape(full_shape[:-1] + (block_num, BLOCK))
    whitened = grid_view / (level_mean[..., None, :, None] + EPSILON)
    return whitened.reshape(full_shape).astype(jnp.bfloat16)


def make_table(total_hours):
    lag_index = lax.iota(jnp.int32, LAGS) - LAGS // 2
    freq_index = lax.iota(jnp.int32, BINS)
    phase_int = jnp.remainder(lag_index[:, None] * freq_index[None, :], 2 * BINS)
    angle_rad = 2.0 * math.pi / (2 * BINS) * phase_int.astype(jnp.float32)
    norm_scale = 1.0 / math.sqrt(BINS * total_hours)
    return jnp.concatenate(
        [jnp.cos(angle_rad) * norm_scale, -jnp.sin(angle_rad) * norm_scale], axis=1
    ).astype(jnp.bfloat16)


def cross_project_kernel(x_ref, y_ref, tre_ref, tim_ref, out_ref, yb_ref, cre_ref, cim_ref):
    step = pl.program_id(0)
    hours = x_ref.shape[0]
    stations = x_ref.shape[2]
    count_src = y_ref.shape[2]
    width = x_ref.shape[3]

    @pl.when(step == 0)
    def _():
        out_ref[...] = jnp.zeros_like(out_ref)

    for h in range(hours):
        for p in range(2):
            for k in range(count_src):
                row = y_ref[h, p, pl.ds(k, 1), :].astype(jnp.float32)
                yb_ref[h, p, k] = jnp.broadcast_to(row, (ROWS, width))

    def body(r, carry):
        first = pl.multiple_of(r * ROWS, ROWS)
        xs = [
            [x_ref[h, p, pl.ds(first, ROWS), :].astype(jnp.float32) for p in range(2)]
            for h in range(hours)
        ]
        for k in range(count_src):
            real = None
            imag = None
            for h in range(hours):
                y0 = yb_ref[h, 0, k]
                y1 = yb_ref[h, 1, k]
                x0, x1 = xs[h]
                re_h = y0 * x0 + y1 * x1
                im_h = y1 * x0 - y0 * x1
                real = re_h if real is None else real + re_h
                imag = im_h if imag is None else imag + im_h
            dest = pl.ds(k * stations + first, ROWS)
            cre_ref[dest, :] = real.astype(jnp.bfloat16)
            cim_ref[dest, :] = imag.astype(jnp.bfloat16)
        return carry

    lax.fori_loop(0, stations // ROWS, body, 0)
    dims = (((1,), (1,)), ((), ()))
    out_ref[...] += lax.dot_general(
        tre_ref[...], cre_ref[...], dims, preferred_element_type=jnp.float32
    ) + lax.dot_general(tim_ref[...], cim_ref[...], dims, preferred_element_type=jnp.float32)


def cross_project(receivers, sources, transform, stations):
    hours, _, _, bins = receivers.shape
    count_src = sources.shape[2]
    lags = transform.shape[0]
    steps = bins // CHUNK
    return pl.pallas_call(
        cross_project_kernel,
        grid=(steps,),
        in_specs=[
            pl.BlockSpec((hours, 2, stations, CHUNK), lambda j: (0, 0, 0, j)),
            pl.BlockSpec((hours, 2, count_src, CHUNK), lambda j: (0, 0, 0, j)),
            pl.BlockSpec((lags, CHUNK), lambda j: (0, j)),
            pl.BlockSpec((lags, CHUNK), lambda j: (0, j + steps)),
        ],
        out_specs=pl.BlockSpec((lags, count_src * stations), lambda j: (0, 0)),
        out_shape=jax.ShapeDtypeStruct((lags, count_src * stations), jnp.float32),
        scratch_shapes=[
            pltpu.VMEM((hours, 2, count_src, ROWS, CHUNK), jnp.float32),
            pltpu.VMEM((count_src * stations, CHUNK), jnp.bfloat16),
            pltpu.VMEM((count_src * stations, CHUNK), jnp.bfloat16),
        ],
        compiler_params=pltpu.CompilerParams(dimension_semantics=("arbitrary",)),
    )(receivers, sources, transform, transform)


def reduce_lags(projected):
    index = lax.axis_index("tm")
    core = index % 2
    z_lo = index // 2
    lags, width = projected.shape
    blocks = projected.reshape(2, 2, lags // 4, width)
    keep = lax.dynamic_index_in_dim(blocks, core, axis=1, keepdims=False)
    send = lax.dynamic_index_in_dim(blocks, 1 - core, axis=1, keepdims=False)
    half = keep + lax.ppermute(send, "tm", perm=[(0, 1), (1, 0), (2, 3), (3, 2)])
    keep = lax.dynamic_index_in_dim(half, z_lo, axis=0, keepdims=False)
    send = lax.dynamic_index_in_dim(half, 1 - z_lo, axis=0, keepdims=False)
    return keep + lax.ppermute(send, "tm", perm=[(0, 2), (2, 0), (1, 3), (3, 1)])


def local(spectra, src_ids):
    hours_dev, stations, _, bins_dev = spectra.shape
    shards = lax.axis_size("sta")
    stations_dev = stations // shards
    flat_ids = src_ids.reshape(-1)
    count_all = flat_ids.shape[0]
    by_part = jnp.transpose(spectra, (0, 2, 1, 3))
    src_raw = jnp.take(by_part, flat_ids, axis=2)
    chunks = by_part.reshape(hours_dev, 2, shards, stations_dev, bins_dev)
    src_copies = jnp.broadcast_to(
        src_raw[:, :, None], (hours_dev, 2, shards, count_all, bins_dev)
    )
    send = jnp.concatenate([chunks, src_copies], axis=3).reshape(
        hours_dev, 2, shards * (stations_dev + count_all), bins_dev
    )
    joined = lax.all_to_all(send, "sta", split_axis=2, concat_axis=3, tiled=True)
    values = joined.astype(jnp.float32)
    magnitude = jnp.sqrt(values[:, 0] * values[:, 0] + values[:, 1] * values[:, 1])
    block_num = BINS // BLOCK
    indicator = (
        lax.broadcasted_iota(jnp.int32, (BINS, block_num), 0) // BLOCK
        == lax.broadcasted_iota(jnp.int32, (BINS, block_num), 1)
    ).astype(jnp.float32)
    totals = jnp.einsum(
        "hrf,fb->hrb", magnitude, indicator, precision=lax.Precision.HIGHEST
    )
    padded = jnp.pad(totals, ((0, 0), (0, 0), (1, 1)))
    level_mean = (padded[..., :-2] + padded[..., 1:-1] + padded[..., 2:]) / (3.0 * BLOCK)
    denom = jnp.einsum(
        "hrb,fb->hrf", level_mean + EPSILON, indicator, precision=lax.Precision.HIGHEST
    )
    white = (values / denom[:, None]).astype(jnp.bfloat16)
    transform = make_table(hours_dev * lax.axis_size("tm"))
    row_count = transform.shape[0] // lax.axis_size("tm")
    results = []
    for step_no in range(ROUNDS):
        first = stations_dev + step_no * NSRC
        sources = white[:, :, first:first + NSRC]
        projected = cross_project(white, sources, transform, stations_dev)
        stacked = reduce_lags(projected)
        results.append(stacked.reshape(row_count, NSRC, stations_dev))
    return jnp.stack(results)


def solution(mesh):
    return jax.shard_map(
        local,
        mesh=mesh,
        in_specs=(P("tm", None, None, "sta"), P()),
        out_specs=P(None, "tm", None, "sta"),
        check_vma=False,
    )
```

```python
import math

import jax
import jax.numpy as jnp
from jax import lax
from jax.experimental import pallas as pl
from jax.experimental.pallas import tpu as pltpu
from jax.sharding import PartitionSpec as P

BINS = 4096
BLOCK = 64
LAGS = 256
NSRC = 8
ROUNDS = 3

CHUNK = 256
ROWS = 16

EPSILON = 1e-05


def block_sums(spec):
    values = spec.astype(jnp.float32)
    magnitude = jnp.sqrt(
        values[..., 0, :] * values[..., 0, :] + values[..., 1, :] * values[..., 1, :]
    )
    full_shape = magnitude.shape
    return magnitude.reshape(full_shape[:-1] + (full_shape[-1] // BLOCK, BLOCK)).sum(axis=-1)


def level_divide(spec, padded):
    block_num = padded.shape[-1] - 2
    level_mean = (padded[..., :-2] + padded[..., 1:-1] + padded[..., 2:]) / (3.0 * BLOCK)
    full_shape = spec.shape
    grid_view = spec.astype(jnp.float32).reshape(full_shape[:-1] + (block_num, BLOCK))
    whitened = grid_view / (level_mean[..., None, :, None] + EPSILON)
    return whitened.reshape(full_shape).astype(jnp.bfloat16)


def make_table(total_hours):
    lag_index = lax.iota(jnp.int32, LAGS) - LAGS // 2
    freq_index = lax.iota(jnp.int32, BINS)
    phase_int = jnp.remainder(lag_index[:, None] * freq_index[None, :], 2 * BINS)
    angle_rad = 2.0 * math.pi / (2 * BINS) * phase_int.astype(jnp.float32)
    norm_scale = 1.0 / math.sqrt(BINS * total_hours)
    return jnp.concatenate(
        [jnp.cos(angle_rad) * norm_scale, -jnp.sin(angle_rad) * norm_scale], axis=1
    ).astype(jnp.bfloat16)


def cross_project_kernel(x_ref, y_ref, tre_ref, tim_ref, out_ref, yb_ref, cre_ref, cim_ref):
    step = pl.program_id(0)
    hours = x_ref.shape[0]
    stations = x_ref.shape[2]
    count_src = y_ref.shape[2]
    width = x_ref.shape[3]

    @pl.when(step == 0)
    def _():
        out_ref[...] = jnp.zeros_like(out_ref)

    for h in range(hours):
        for p in range(2):
            for k in range(count_src):
                row = y_ref[h, p, pl.ds(k, 1), :].astype(jnp.float32)
                yb_ref[h, p, k] = jnp.broadcast_to(row, (ROWS, width))

    def body(r, carry):
        first = pl.multiple_of(r * ROWS, ROWS)
        xs = [
            [x_ref[h, p, pl.ds(first, ROWS), :].astype(jnp.float32) for p in range(2)]
            for h in range(hours)
        ]
        for k in range(count_src):
            real = None
            imag = None
            for h in range(hours):
                y0 = yb_ref[h, 0, k]
                y1 = yb_ref[h, 1, k]
                x0, x1 = xs[h]
                re_h = y0 * x0 + y1 * x1
                im_h = y1 * x0 - y0 * x1
                real = re_h if real is None else real + re_h
                imag = im_h if imag is None else imag + im_h
            dest = pl.ds(k * stations + first, ROWS)
            cre_ref[dest, :] = real.astype(jnp.bfloat16)
            cim_ref[dest, :] = imag.astype(jnp.bfloat16)
        return carry

    lax.fori_loop(0, stations // ROWS, body, 0)
    dims = (((1,), (1,)), ((), ()))
    out_ref[...] += lax.dot_general(
        tre_ref[...], cre_ref[...], dims, preferred_element_type=jnp.float32
    ) + lax.dot_general(tim_ref[...], cim_ref[...], dims, preferred_element_type=jnp.float32)


def cross_project(receivers, sources, transform, stations):
    hours, _, _, bins = receivers.shape
    count_src = sources.shape[2]
    lags = transform.shape[0]
    steps = bins // CHUNK
    return pl.pallas_call(
        cross_project_kernel,
        grid=(steps,),
        in_specs=[
            pl.BlockSpec((hours, 2, stations, CHUNK), lambda j: (0, 0, 0, j)),
            pl.BlockSpec((hours, 2, count_src, CHUNK), lambda j: (0, 0, 0, j)),
            pl.BlockSpec((lags, CHUNK), lambda j: (0, j)),
            pl.BlockSpec((lags, CHUNK), lambda j: (0, j + steps)),
        ],
        out_specs=pl.BlockSpec((lags, count_src * stations), lambda j: (0, 0)),
        out_shape=jax.ShapeDtypeStruct((lags, count_src * stations), jnp.float32),
        scratch_shapes=[
            pltpu.VMEM((hours, 2, count_src, ROWS, CHUNK), jnp.float32),
            pltpu.VMEM((count_src * stations, CHUNK), jnp.bfloat16),
            pltpu.VMEM((count_src * stations, CHUNK), jnp.bfloat16),
        ],
        compiler_params=pltpu.CompilerParams(dimension_semantics=("arbitrary",)),
    )(receivers, sources, transform, transform)


def reduce_lags(projected):
    index = lax.axis_index("tm")
    core = index % 2
    z_lo = index // 2
    lags, width = projected.shape
    blocks = projected.reshape(2, 2, lags // 4, width)
    keep = lax.dynamic_index_in_dim(blocks, core, axis=1, keepdims=False)
    send = lax.dynamic_index_in_dim(blocks, 1 - core, axis=1, keepdims=False)
    half = keep + lax.ppermute(send, "tm", perm=[(0, 1), (1, 0), (2, 3), (3, 2)])
    keep = lax.dynamic_index_in_dim(half, z_lo, axis=0, keepdims=False)
    send = lax.dynamic_index_in_dim(half, 1 - z_lo, axis=0, keepdims=False)
    return keep + lax.ppermute(send, "tm", perm=[(0, 2), (2, 0), (1, 3), (3, 1)])


def whiten(joined):
    hours_dev = joined.shape[0]
    values = joined.astype(jnp.float32)
    magnitude = jnp.sqrt(values[:, 0] * values[:, 0] + values[:, 1] * values[:, 1])
    block_num = BINS // BLOCK
    indicator = (
        lax.broadcasted_iota(jnp.int32, (BINS, block_num), 0) // BLOCK
        == lax.broadcasted_iota(jnp.int32, (BINS, block_num), 1)
    ).astype(jnp.float32)
    totals = jnp.einsum(
        "hrf,fb->hrb", magnitude, indicator, precision=lax.Precision.HIGHEST
    )
    padded = jnp.pad(totals, ((0, 0), (0, 0), (1, 1)))
    level_mean = (padded[..., :-2] + padded[..., 1:-1] + padded[..., 2:]) / (3.0 * BLOCK)
    denom = jnp.einsum(
        "hrb,fb->hrf", level_mean + EPSILON, indicator, precision=lax.Precision.HIGHEST
    )
    return (values / denom[:, None]).astype(jnp.bfloat16)


def local(spectra, src_ids):
    hours_dev, stations, _, bins_dev = spectra.shape
    shards = lax.axis_size("sta")
    stations_dev = stations // shards
    half = stations_dev // 2
    flat_ids = src_ids.reshape(-1)
    count_all = flat_ids.shape[0]
    by_part = jnp.transpose(spectra, (0, 2, 1, 3))
    src_raw = jnp.take(by_part, flat_ids, axis=2)
    chunks = by_part.reshape(hours_dev, 2, shards, stations_dev, bins_dev)
    src_copies = jnp.broadcast_to(
        src_raw[:, :, None], (hours_dev, 2, shards, count_all, bins_dev)
    )
    send_a = jnp.concatenate([chunks[:, :, :, :half], src_copies], axis=3).reshape(
        hours_dev, 2, shards * (half + count_all), bins_dev
    )
    send_b = chunks[:, :, :, half:].reshape(hours_dev, 2, shards * half, bins_dev)
    joined_a = lax.all_to_all(send_a, "sta", split_axis=2, concat_axis=3, tiled=True)
    send_b, joined_a = lax.optimization_barrier((send_b, joined_a))
    joined_b = lax.all_to_all(send_b, "sta", split_axis=2, concat_axis=3, tiled=True)
    white_a = whiten(joined_a)
    transform = make_table(hours_dev * lax.axis_size("tm"))
    row_count = transform.shape[0] // lax.axis_size("tm")
    sources = [
        white_a[:, :, half + step_no * NSRC:half + (step_no + 1) * NSRC]
        for step_no in range(ROUNDS)
    ]
    parts_a = [
        reduce_lags(cross_project(white_a, sources[step_no], transform, half))
        for step_no in range(ROUNDS)
    ]
    white_b = whiten(joined_b)
    parts_b = [
        reduce_lags(cross_project(white_b, sources[step_no], transform, half))
        for step_no in range(ROUNDS)
    ]
    results = [
        jnp.concatenate(
            [
                parts_a[step_no].reshape(row_count, NSRC, half),
                parts_b[step_no].reshape(row_count, NSRC, half),
            ],
            axis=2,
        )
        for step_no in range(ROUNDS)
    ]
    return jnp.stack(results)


def solution(mesh):
    return jax.shard_map(
        local,
        mesh=mesh,
        in_specs=(P("tm", None, None, "sta"), P()),
        out_specs=P(None, "tm", None, "sta"),
        check_vma=False,
    )
```

```python
import math

import jax
import jax.numpy as jnp
from jax import lax
from jax.experimental import pallas as pl
from jax.experimental.pallas import tpu as pltpu
from jax.sharding import PartitionSpec as P

BINS = 4096
BLOCK = 64
LAGS = 256
NSRC = 8
ROUNDS = 3

CHUNK = 256
ROWS = 16

EPSILON = 1e-05


def block_sums(spec):
    values = spec.astype(jnp.float32)
    magnitude = jnp.sqrt(
        values[..., 0, :] * values[..., 0, :] + values[..., 1, :] * values[..., 1, :]
    )
    full_shape = magnitude.shape
    return magnitude.reshape(full_shape[:-1] + (full_shape[-1] // BLOCK, BLOCK)).sum(axis=-1)


def level_divide(spec, padded):
    block_num = padded.shape[-1] - 2
    level_mean = (padded[..., :-2] + padded[..., 1:-1] + padded[..., 2:]) / (3.0 * BLOCK)
    full_shape = spec.shape
    grid_view = spec.astype(jnp.float32).reshape(full_shape[:-1] + (block_num, BLOCK))
    whitened = grid_view / (level_mean[..., None, :, None] + EPSILON)
    return whitened.reshape(full_shape).astype(jnp.bfloat16)


def make_table(total_hours):
    lag_index = lax.iota(jnp.int32, LAGS) - LAGS // 2
    freq_index = lax.iota(jnp.int32, BINS)
    phase_int = jnp.remainder(lag_index[:, None] * freq_index[None, :], 2 * BINS)
    angle_rad = 2.0 * math.pi / (2 * BINS) * phase_int.astype(jnp.float32)
    norm_scale = 1.0 / math.sqrt(BINS * total_hours)
    return jnp.concatenate(
        [jnp.cos(angle_rad) * norm_scale, -jnp.sin(angle_rad) * norm_scale], axis=1
    ).astype(jnp.bfloat16)


def cross_project_kernel(x_ref, y_ref, tre_ref, tim_ref, out_ref, yb_ref, cre_ref, cim_ref):
    step = pl.program_id(0)
    hours = x_ref.shape[0]
    stations = x_ref.shape[2]
    count_src = y_ref.shape[2]
    width = x_ref.shape[3]

    @pl.when(step == 0)
    def _():
        out_ref[...] = jnp.zeros_like(out_ref)

    for h in range(hours):
        for p in range(2):
            for k in range(count_src):
                row = y_ref[h, p, pl.ds(k, 1), :].astype(jnp.float32)
                yb_ref[h, p, k] = jnp.broadcast_to(row, (ROWS, width))

    def body(r, carry):
        first = pl.multiple_of(r * ROWS, ROWS)
        xs = [
            [x_ref[h, p, pl.ds(first, ROWS), :].astype(jnp.float32) for p in range(2)]
            for h in range(hours)
        ]
        for k in range(count_src):
            real = None
            imag = None
            for h in range(hours):
                y0 = yb_ref[h, 0, k]
                y1 = yb_ref[h, 1, k]
                x0, x1 = xs[h]
                re_h = y0 * x0 + y1 * x1
                im_h = y1 * x0 - y0 * x1
                real = re_h if real is None else real + re_h
                imag = im_h if imag is None else imag + im_h
            dest = pl.ds(k * stations + first, ROWS)
            cre_ref[dest, :] = real.astype(jnp.bfloat16)
            cim_ref[dest, :] = imag.astype(jnp.bfloat16)
        return carry

    lax.fori_loop(0, stations // ROWS, body, 0)
    dims = (((1,), (1,)), ((), ()))
    span = NSRC * stations
    for rnd in range(count_src // NSRC):
        cols = pl.ds(rnd * span, span)
        out_ref[:, cols] += lax.dot_general(
            tre_ref[...], cre_ref[cols, :], dims, preferred_element_type=jnp.float32
        ) + lax.dot_general(tim_ref[...], cim_ref[cols, :], dims, preferred_element_type=jnp.float32)


def cross_project(receivers, sources, transform, stations):
    hours, _, _, bins = receivers.shape
    count_src = sources.shape[2]
    lags = transform.shape[0]
    steps = bins // CHUNK
    return pl.pallas_call(
        cross_project_kernel,
        grid=(steps,),
        in_specs=[
            pl.BlockSpec((hours, 2, stations, CHUNK), lambda j: (0, 0, 0, j)),
            pl.BlockSpec((hours, 2, count_src, CHUNK), lambda j: (0, 0, 0, j)),
            pl.BlockSpec((lags, CHUNK), lambda j: (0, j)),
            pl.BlockSpec((lags, CHUNK), lambda j: (0, j + steps)),
        ],
        out_specs=pl.BlockSpec((lags, count_src * stations), lambda j: (0, 0)),
        out_shape=jax.ShapeDtypeStruct((lags, count_src * stations), jnp.float32),
        scratch_shapes=[
            pltpu.VMEM((hours, 2, count_src, ROWS, CHUNK), jnp.float32),
            pltpu.VMEM((count_src * stations, CHUNK), jnp.bfloat16),
            pltpu.VMEM((count_src * stations, CHUNK), jnp.bfloat16),
        ],
        compiler_params=pltpu.CompilerParams(dimension_semantics=("arbitrary",)),
    )(receivers, sources, transform, transform)


def reduce_lags(projected):
    index = lax.axis_index("tm")
    core = index % 2
    z_lo = index // 2
    lags, width = projected.shape
    blocks = projected.reshape(2, 2, lags // 4, width)
    keep = lax.dynamic_index_in_dim(blocks, core, axis=1, keepdims=False)
    send = lax.dynamic_index_in_dim(blocks, 1 - core, axis=1, keepdims=False)
    half = keep + lax.ppermute(send, "tm", perm=[(0, 1), (1, 0), (2, 3), (3, 2)])
    keep = lax.dynamic_index_in_dim(half, z_lo, axis=0, keepdims=False)
    send = lax.dynamic_index_in_dim(half, 1 - z_lo, axis=0, keepdims=False)
    return keep + lax.ppermute(send, "tm", perm=[(0, 2), (2, 0), (1, 3), (3, 1)])


def whiten(joined):
    hours_dev = joined.shape[0]
    values = joined.astype(jnp.float32)
    magnitude = jnp.sqrt(values[:, 0] * values[:, 0] + values[:, 1] * values[:, 1])
    block_num = BINS // BLOCK
    indicator = (
        lax.broadcasted_iota(jnp.int32, (BINS, block_num), 0) // BLOCK
        == lax.broadcasted_iota(jnp.int32, (BINS, block_num), 1)
    ).astype(jnp.float32)
    totals = jnp.einsum(
        "hrf,fb->hrb", magnitude, indicator, precision=lax.Precision.HIGHEST
    )
    padded = jnp.pad(totals, ((0, 0), (0, 0), (1, 1)))
    level_mean = (padded[..., :-2] + padded[..., 1:-1] + padded[..., 2:]) / (3.0 * BLOCK)
    denom = jnp.einsum(
        "hrb,fb->hrf", level_mean + EPSILON, indicator, precision=lax.Precision.HIGHEST
    )
    return (values / denom[:, None]).astype(jnp.bfloat16)


def local(spectra, src_ids):
    hours_dev, stations, _, bins_dev = spectra.shape
    shards = lax.axis_size("sta")
    stations_dev = stations // shards
    half = stations_dev // 2
    flat_ids = src_ids.reshape(-1)
    count_all = flat_ids.shape[0]
    by_part = jnp.transpose(spectra, (0, 2, 1, 3))
    src_raw = jnp.take(by_part, flat_ids, axis=2)
    chunks = by_part.reshape(hours_dev, 2, shards, stations_dev, bins_dev)
    src_copies = jnp.broadcast_to(
        src_raw[:, :, None], (hours_dev, 2, shards, count_all, bins_dev)
    )
    send_a = jnp.concatenate([chunks[:, :, :, :half], src_copies], axis=3).reshape(
        hours_dev, 2, shards * (half + count_all), bins_dev
    )
    send_b = chunks[:, :, :, half:].reshape(hours_dev, 2, shards * half, bins_dev)
    joined_a = lax.all_to_all(send_a, "sta", split_axis=2, concat_axis=3, tiled=True)
    send_b, joined_a = lax.optimization_barrier((send_b, joined_a))
    joined_b = lax.all_to_all(send_b, "sta", split_axis=2, concat_axis=3, tiled=True)
    white_a = whiten(joined_a)
    transform = make_table(hours_dev * lax.axis_size("tm"))
    row_count = transform.shape[0] // lax.axis_size("tm")
    sources = white_a[:, :, half:half + count_all]
    part_a = reduce_lags(cross_project(white_a, sources, transform, half))
    white_b = whiten(joined_b)
    part_b = reduce_lags(cross_project(white_b, sources, transform, half))
    both = jnp.concatenate(
        [
            part_a.reshape(row_count, ROUNDS, NSRC, half),
            part_b.reshape(row_count, ROUNDS, NSRC, half),
        ],
        axis=3,
    )
    return jnp.transpose(both, (1, 0, 2, 3))


def solution(mesh):
    return jax.shard_map(
        local,
        mesh=mesh,
        in_specs=(P("tm", None, None, "sta"), P()),
        out_specs=P(None, "tm", None, "sta"),
        check_vma=False,
    )
```

```python
import math

import jax
import jax.numpy as jnp
from jax import lax
from jax.experimental import pallas as pl
from jax.experimental.pallas import tpu as pltpu
from jax.sharding import PartitionSpec as P

BINS = 4096
BLOCK = 64
LAGS = 256
NSRC = 8
ROUNDS = 3

CHUNK = 512
ROWS = 16

EPSILON = 1e-05


def block_sums(spec):
    values = spec.astype(jnp.float32)
    magnitude = jnp.sqrt(
        values[..., 0, :] * values[..., 0, :] + values[..., 1, :] * values[..., 1, :]
    )
    full_shape = magnitude.shape
    return magnitude.reshape(full_shape[:-1] + (full_shape[-1] // BLOCK, BLOCK)).sum(axis=-1)


def level_divide(spec, padded):
    block_num = padded.shape[-1] - 2
    level_mean = (padded[..., :-2] + padded[..., 1:-1] + padded[..., 2:]) / (3.0 * BLOCK)
    full_shape = spec.shape
    grid_view = spec.astype(jnp.float32).reshape(full_shape[:-1] + (block_num, BLOCK))
    whitened = grid_view / (level_mean[..., None, :, None] + EPSILON)
    return whitened.reshape(full_shape).astype(jnp.bfloat16)


def make_table(total_hours):
    lag_index = lax.iota(jnp.int32, LAGS) - LAGS // 2
    freq_index = lax.iota(jnp.int32, BINS)
    phase_int = jnp.remainder(lag_index[:, None] * freq_index[None, :], 2 * BINS)
    angle_rad = 2.0 * math.pi / (2 * BINS) * phase_int.astype(jnp.float32)
    norm_scale = 1.0 / math.sqrt(BINS * total_hours)
    return jnp.concatenate(
        [jnp.cos(angle_rad) * norm_scale, -jnp.sin(angle_rad) * norm_scale], axis=1
    ).astype(jnp.bfloat16)


def cross_project_kernel(x_ref, y_ref, tre_ref, tim_ref, out_ref, yb_ref, cre_ref, cim_ref):
    step = pl.program_id(0)
    hours = x_ref.shape[0]
    stations = x_ref.shape[2]
    count_src = y_ref.shape[2]
    width = x_ref.shape[3]

    @pl.when(step == 0)
    def _():
        out_ref[...] = jnp.zeros_like(out_ref)

    for h in range(hours):
        for p in range(2):
            for k in range(count_src):
                row = y_ref[h, p, pl.ds(k, 1), :].astype(jnp.float32)
                yb_ref[h, p, k] = jnp.broadcast_to(row, (ROWS, width))

    def body(r, carry):
        first = pl.multiple_of(r * ROWS, ROWS)
        xs = [
            [x_ref[h, p, pl.ds(first, ROWS), :].astype(jnp.float32) for p in range(2)]
            for h in range(hours)
        ]
        for k in range(count_src):
            real = None
            imag = None
            for h in range(hours):
                y0 = yb_ref[h, 0, k]
                y1 = yb_ref[h, 1, k]
                x0, x1 = xs[h]
                re_h = y0 * x0 + y1 * x1
                im_h = y1 * x0 - y0 * x1
                real = re_h if real is None else real + re_h
                imag = im_h if imag is None else imag + im_h
            dest = pl.ds(k * stations + first, ROWS)
            cre_ref[dest, :] = real.astype(jnp.bfloat16)
            cim_ref[dest, :] = imag.astype(jnp.bfloat16)
        return carry

    lax.fori_loop(0, stations // ROWS, body, 0)
    dims = (((1,), (1,)), ((), ()))
    span = NSRC * stations
    for rnd in range(count_src // NSRC):
        cols = pl.ds(rnd * span, span)
        out_ref[:, cols] += lax.dot_general(
            tre_ref[...], cre_ref[cols, :], dims, preferred_element_type=jnp.float32
        ) + lax.dot_general(tim_ref[...], cim_ref[cols, :], dims, preferred_element_type=jnp.float32)


def cross_project(receivers, sources, transform, stations):
    hours, _, _, bins = receivers.shape
    count_src = sources.shape[2]
    lags = transform.shape[0]
    steps = bins // CHUNK
    return pl.pallas_call(
        cross_project_kernel,
        grid=(steps,),
        in_specs=[
            pl.BlockSpec((hours, 2, stations, CHUNK), lambda j: (0, 0, 0, j)),
            pl.BlockSpec((hours, 2, count_src, CHUNK), lambda j: (0, 0, 0, j)),
            pl.BlockSpec((lags, CHUNK), lambda j: (0, j)),
            pl.BlockSpec((lags, CHUNK), lambda j: (0, j + steps)),
        ],
        out_specs=pl.BlockSpec((lags, count_src * stations), lambda j: (0, 0)),
        out_shape=jax.ShapeDtypeStruct((lags, count_src * stations), jnp.float32),
        scratch_shapes=[
            pltpu.VMEM((hours, 2, count_src, ROWS, CHUNK), jnp.float32),
            pltpu.VMEM((count_src * stations, CHUNK), jnp.bfloat16),
            pltpu.VMEM((count_src * stations, CHUNK), jnp.bfloat16),
        ],
        compiler_params=pltpu.CompilerParams(dimension_semantics=("arbitrary",)),
    )(receivers, sources, transform, transform)


def reduce_lags(projected):
    index = lax.axis_index("tm")
    core = index % 2
    z_lo = index // 2
    lags, width = projected.shape
    blocks = projected.reshape(2, 2, lags // 4, width)
    keep = lax.dynamic_index_in_dim(blocks, core, axis=1, keepdims=False)
    send = lax.dynamic_index_in_dim(blocks, 1 - core, axis=1, keepdims=False)
    half = keep + lax.ppermute(send, "tm", perm=[(0, 1), (1, 0), (2, 3), (3, 2)])
    keep = lax.dynamic_index_in_dim(half, z_lo, axis=0, keepdims=False)
    send = lax.dynamic_index_in_dim(half, 1 - z_lo, axis=0, keepdims=False)
    return keep + lax.ppermute(send, "tm", perm=[(0, 2), (2, 0), (1, 3), (3, 1)])


def whiten(joined):
    hours_dev = joined.shape[0]
    values = joined.astype(jnp.float32)
    magnitude = jnp.sqrt(values[:, 0] * values[:, 0] + values[:, 1] * values[:, 1])
    block_num = BINS // BLOCK
    indicator = (
        lax.broadcasted_iota(jnp.int32, (BINS, block_num), 0) // BLOCK
        == lax.broadcasted_iota(jnp.int32, (BINS, block_num), 1)
    ).astype(jnp.float32)
    totals = jnp.einsum(
        "hrf,fb->hrb", magnitude, indicator, precision=lax.Precision.HIGHEST
    )
    padded = jnp.pad(totals, ((0, 0), (0, 0), (1, 1)))
    level_mean = (padded[..., :-2] + padded[..., 1:-1] + padded[..., 2:]) / (3.0 * BLOCK)
    denom = jnp.einsum(
        "hrb,fb->hrf", level_mean + EPSILON, indicator, precision=lax.Precision.HIGHEST
    )
    return (values / denom[:, None]).astype(jnp.bfloat16)


def local(spectra, src_ids):
    hours_dev, stations, _, bins_dev = spectra.shape
    shards = lax.axis_size("sta")
    stations_dev = stations // shards
    half = stations_dev // 2
    flat_ids = src_ids.reshape(-1)
    count_all = flat_ids.shape[0]
    by_part = jnp.transpose(spectra, (0, 2, 1, 3))
    src_raw = jnp.take(by_part, flat_ids, axis=2)
    chunks = by_part.reshape(hours_dev, 2, shards, stations_dev, bins_dev)
    src_copies = jnp.broadcast_to(
        src_raw[:, :, None], (hours_dev, 2, shards, count_all, bins_dev)
    )
    send_a = jnp.concatenate([chunks[:, :, :, :half], src_copies], axis=3).reshape(
        hours_dev, 2, shards * (half + count_all), bins_dev
    )
    send_b = chunks[:, :, :, half:].reshape(hours_dev, 2, shards * half, bins_dev)
    joined_a = lax.all_to_all(send_a, "sta", split_axis=2, concat_axis=3, tiled=True)
    send_b, joined_a = lax.optimization_barrier((send_b, joined_a))
    joined_b = lax.all_to_all(send_b, "sta", split_axis=2, concat_axis=3, tiled=True)
    white_a = whiten(joined_a)
    transform = make_table(hours_dev * lax.axis_size("tm"))
    row_count = transform.shape[0] // lax.axis_size("tm")
    sources = white_a[:, :, half:half + count_all]
    part_a = reduce_lags(cross_project(white_a, sources, transform, half))
    white_b = whiten(joined_b)
    part_b = reduce_lags(cross_project(white_b, sources, transform, half))
    both = jnp.concatenate(
        [
            part_a.reshape(row_count, ROUNDS, NSRC, half),
            part_b.reshape(row_count, ROUNDS, NSRC, half),
        ],
        axis=3,
    )
    return jnp.transpose(both, (1, 0, 2, 3))


def solution(mesh):
    return jax.shard_map(
        local,
        mesh=mesh,
        in_specs=(P("tm", None, None, "sta"), P()),
        out_specs=P(None, "tm", None, "sta"),
        check_vma=False,
    )
```

```python
import math

import jax
import jax.numpy as jnp
from jax import lax
from jax.experimental import pallas as pl
from jax.experimental.pallas import tpu as pltpu
from jax.sharding import PartitionSpec as P

BINS = 4096
BLOCK = 64
LAGS = 256
NSRC = 8
ROUNDS = 3

CHUNK = 512
ROWS = 16

EPSILON = 1e-05


def block_sums(spec):
    values = spec.astype(jnp.float32)
    magnitude = jnp.sqrt(
        values[..., 0, :] * values[..., 0, :] + values[..., 1, :] * values[..., 1, :]
    )
    full_shape = magnitude.shape
    return magnitude.reshape(full_shape[:-1] + (full_shape[-1] // BLOCK, BLOCK)).sum(axis=-1)


def level_divide(spec, padded):
    block_num = padded.shape[-1] - 2
    level_mean = (padded[..., :-2] + padded[..., 1:-1] + padded[..., 2:]) / (3.0 * BLOCK)
    full_shape = spec.shape
    grid_view = spec.astype(jnp.float32).reshape(full_shape[:-1] + (block_num, BLOCK))
    whitened = grid_view / (level_mean[..., None, :, None] + EPSILON)
    return whitened.reshape(full_shape).astype(jnp.bfloat16)


def make_table(total_hours):
    lag_index = lax.iota(jnp.int32, LAGS) - LAGS // 2
    freq_index = lax.iota(jnp.int32, BINS)
    phase_int = jnp.remainder(lag_index[:, None] * freq_index[None, :], 2 * BINS)
    angle_rad = 2.0 * math.pi / (2 * BINS) * phase_int.astype(jnp.float32)
    norm_scale = 1.0 / math.sqrt(BINS * total_hours)
    return jnp.concatenate(
        [jnp.cos(angle_rad) * norm_scale, -jnp.sin(angle_rad) * norm_scale], axis=1
    ).astype(jnp.bfloat16)


def cross_project_kernel(x_ref, y_ref, tre_ref, tim_ref, out_ref, yb_ref, cre_ref, cim_ref):
    step = pl.program_id(0)
    hours = x_ref.shape[0]
    stations = x_ref.shape[2]
    count_src = y_ref.shape[2]
    width = x_ref.shape[3]

    @pl.when(step == 0)
    def _():
        out_ref[...] = jnp.zeros_like(out_ref)

    for h in range(hours):
        for p in range(2):
            for k in range(count_src):
                row = y_ref[h, p, pl.ds(k, 1), :].astype(jnp.float32)
                yb_ref[h, p, k] = jnp.broadcast_to(row, (ROWS, width))

    def body(r, carry):
        first = pl.multiple_of(r * ROWS, ROWS)
        xs = [
            [x_ref[h, p, pl.ds(first, ROWS), :].astype(jnp.float32) for p in range(2)]
            for h in range(hours)
        ]
        for k in range(count_src):
            real = None
            imag = None
            for h in range(hours):
                y0 = yb_ref[h, 0, k]
                y1 = yb_ref[h, 1, k]
                x0, x1 = xs[h]
                re_h = y0 * x0 + y1 * x1
                im_h = y1 * x0 - y0 * x1
                real = re_h if real is None else real + re_h
                imag = im_h if imag is None else imag + im_h
            dest = pl.ds(k * stations + first, ROWS)
            cre_ref[dest, :] = real.astype(jnp.bfloat16)
            cim_ref[dest, :] = imag.astype(jnp.bfloat16)
        return carry

    lax.fori_loop(0, stations // ROWS, body, 0)
    dims = (((1,), (1,)), ((), ()))
    span = NSRC * stations
    for rnd in range(count_src // NSRC):
        cols = pl.ds(rnd * span, span)
        out_ref[:, cols] += lax.dot_general(
            tre_ref[...], cre_ref[cols, :], dims, preferred_element_type=jnp.float32
        ) + lax.dot_general(tim_ref[...], cim_ref[cols, :], dims, preferred_element_type=jnp.float32)


def cross_project(receivers, sources, transform, stations):
    hours, _, _, bins = receivers.shape
    count_src = sources.shape[2]
    lags = transform.shape[0]
    steps = bins // CHUNK
    return pl.pallas_call(
        cross_project_kernel,
        grid=(steps,),
        in_specs=[
            pl.BlockSpec((hours, 2, stations, CHUNK), lambda j: (0, 0, 0, j)),
            pl.BlockSpec((hours, 2, count_src, CHUNK), lambda j: (0, 0, 0, j)),
            pl.BlockSpec((lags, CHUNK), lambda j: (0, j)),
            pl.BlockSpec((lags, CHUNK), lambda j: (0, j + steps)),
        ],
        out_specs=pl.BlockSpec((lags, count_src * stations), lambda j: (0, 0)),
        out_shape=jax.ShapeDtypeStruct((lags, count_src * stations), jnp.float32),
        scratch_shapes=[
            pltpu.VMEM((hours, 2, count_src, ROWS, CHUNK), jnp.float32),
            pltpu.VMEM((count_src * stations, CHUNK), jnp.bfloat16),
            pltpu.VMEM((count_src * stations, CHUNK), jnp.bfloat16),
        ],
        compiler_params=pltpu.CompilerParams(dimension_semantics=("arbitrary",)),
    )(receivers, sources, transform, transform)


def reduce_lags(projected):
    index = lax.axis_index("tm")
    core = index % 2
    z_lo = index // 2
    lags, width = projected.shape
    blocks = projected.reshape(2, 2, lags // 4, width)
    keep = lax.dynamic_index_in_dim(blocks, core, axis=1, keepdims=False)
    send = lax.dynamic_index_in_dim(blocks, 1 - core, axis=1, keepdims=False)
    half = keep + lax.ppermute(send, "tm", perm=[(0, 1), (1, 0), (2, 3), (3, 2)])
    keep = lax.dynamic_index_in_dim(half, z_lo, axis=0, keepdims=False)
    send = lax.dynamic_index_in_dim(half, 1 - z_lo, axis=0, keepdims=False)
    return keep + lax.ppermute(send, "tm", perm=[(0, 2), (2, 0), (1, 3), (3, 1)])


def whiten(joined):
    hours_dev = joined.shape[0]
    values = joined.astype(jnp.float32)
    magnitude = jnp.sqrt(values[:, 0] * values[:, 0] + values[:, 1] * values[:, 1])
    block_num = BINS // BLOCK
    indicator = (
        lax.broadcasted_iota(jnp.int32, (BINS, block_num), 0) // BLOCK
        == lax.broadcasted_iota(jnp.int32, (BINS, block_num), 1)
    ).astype(jnp.float32)
    totals = jnp.einsum(
        "hrf,fb->hrb", magnitude, indicator, precision=lax.Precision.HIGHEST
    )
    padded = jnp.pad(totals, ((0, 0), (0, 0), (1, 1)))
    level_mean = (padded[..., :-2] + padded[..., 1:-1] + padded[..., 2:]) / (3.0 * BLOCK)
    denom = jnp.einsum(
        "hrb,fb->hrf", level_mean + EPSILON, indicator, precision=lax.Precision.HIGHEST
    )
    return (values / denom[:, None]).astype(jnp.bfloat16)


def to_send(spectra, first, count, extra):
    hours_dev, stations, _, bins_dev = spectra.shape
    shards = lax.axis_size("sta")
    chunks = spectra.reshape(hours_dev, shards, stations // shards, 2, bins_dev)
    chunks = jnp.transpose(chunks[:, :, first:first + count], (0, 3, 1, 2, 4))
    if extra is not None:
        copies = jnp.broadcast_to(
            extra[:, :, None], (hours_dev, 2, shards, extra.shape[2], bins_dev)
        )
        chunks = jnp.concatenate([chunks, copies], axis=3)
    return chunks.reshape(hours_dev, 2, -1, bins_dev)


def local(spectra, src_ids):
    hours_dev, stations, _, bins_dev = spectra.shape
    shards = lax.axis_size("sta")
    stations_dev = stations // shards
    half = stations_dev // 2
    flat_ids = src_ids.reshape(-1)
    count_all = flat_ids.shape[0]
    src_raw = jnp.transpose(jnp.take(spectra, flat_ids, axis=1), (0, 2, 1, 3))
    send_a = to_send(spectra, 0, half, src_raw)
    joined_a = lax.all_to_all(send_a, "sta", split_axis=2, concat_axis=3, tiled=True)
    transform = make_table(hours_dev * lax.axis_size("tm"))
    spectra_b, transform = lax.optimization_barrier((spectra, transform))
    send_b = to_send(spectra_b, half, stations_dev - half, None)
    send_b, joined_a = lax.optimization_barrier((send_b, joined_a))
    joined_b = lax.all_to_all(send_b, "sta", split_axis=2, concat_axis=3, tiled=True)
    white_a = whiten(joined_a)
    row_count = transform.shape[0] // lax.axis_size("tm")
    sources = white_a[:, :, half:half + count_all]
    part_a = reduce_lags(cross_project(white_a, sources, transform, half))
    white_b = whiten(joined_b)
    split = (ROUNDS - 1) * NSRC
    part_b1 = reduce_lags(cross_project(white_b, sources[:, :, :split], transform, half))
    part_b2 = reduce_lags(cross_project(white_b, sources[:, :, split:], transform, half))
    part_b = jnp.concatenate(
        [
            part_b1.reshape(row_count, ROUNDS - 1, NSRC, half),
            part_b2.reshape(row_count, 1, NSRC, half),
        ],
        axis=1,
    )
    both = jnp.concatenate(
        [part_a.reshape(row_count, ROUNDS, NSRC, half), part_b], axis=3
    )
    return jnp.transpose(both, (1, 0, 2, 3))


def solution(mesh):
    return jax.shard_map(
        local,
        mesh=mesh,
        in_specs=(P("tm", None, None, "sta"), P()),
        out_specs=P(None, "tm", None, "sta"),
        check_vma=False,
    )
```

```python
import math

import jax
import jax.numpy as jnp
from jax import lax
from jax.experimental import pallas as pl
from jax.experimental.pallas import tpu as pltpu
from jax.sharding import PartitionSpec as P


BINS = 4096
BLOCK = 64
LAGS = 256
NSRC = 8
ROUNDS = 3

CHUNK = 512
ROWS = 16

EPSILON = 1e-05


def make_table(total_hours):
    lag_index = lax.iota(jnp.int32, LAGS) - LAGS // 2
    freq_index = lax.iota(jnp.int32, BINS)
    phase_int = jnp.remainder(lag_index[:, None] * freq_index[None, :], 2 * BINS)
    angle_rad = 2.0 * math.pi / (2 * BINS) * phase_int.astype(jnp.float32)
    norm_scale = 1.0 / math.sqrt(BINS * total_hours)
    return jnp.concatenate(
        [jnp.cos(angle_rad) * norm_scale, -jnp.sin(angle_rad) * norm_scale], axis=1
    ).astype(jnp.bfloat16)


def cross_project_kernel(x_ref, y_ref, tre_ref, tim_ref, out_ref, yb_ref, cre_ref, cim_ref):
    step = pl.program_id(0)
    hours = x_ref.shape[0]
    stations = x_ref.shape[2]
    count_src = y_ref.shape[2]
    width = x_ref.shape[3]

    @pl.when(step == 0)
    def _():
        out_ref[...] = jnp.zeros_like(out_ref)

    for h in range(hours):
        for p in range(2):
            for k in range(count_src):
                row = y_ref[h, p, pl.ds(k, 1), :].astype(jnp.float32)
                yb_ref[h, p, k] = jnp.broadcast_to(row, (ROWS, width))

    def body(r, carry):
        first = pl.multiple_of(r * ROWS, ROWS)
        xs = [
            [x_ref[h, p, pl.ds(first, ROWS), :].astype(jnp.float32) for p in range(2)]
            for h in range(hours)
        ]
        for k in range(count_src):
            real = None
            imag = None
            for h in range(hours):
                y0 = yb_ref[h, 0, k]
                y1 = yb_ref[h, 1, k]
                x0, x1 = xs[h]
                re_h = y0 * x0 + y1 * x1
                im_h = y1 * x0 - y0 * x1
                real = re_h if real is None else real + re_h
                imag = im_h if imag is None else imag + im_h
            dest = pl.ds(k * stations + first, ROWS)
            cre_ref[dest, :] = real.astype(jnp.bfloat16)
            cim_ref[dest, :] = imag.astype(jnp.bfloat16)
        return carry

    lax.fori_loop(0, stations // ROWS, body, 0)
    dims = (((1,), (1,)), ((), ()))
    span = NSRC * stations
    for rnd in range(count_src // NSRC):
        cols = pl.ds(rnd * span, span)
        out_ref[:, cols] += lax.dot_general(
            tre_ref[...], cre_ref[cols, :], dims, preferred_element_type=jnp.float32
        ) + lax.dot_general(tim_ref[...], cim_ref[cols, :], dims, preferred_element_type=jnp.float32)


def cross_project(receivers, sources, transform, stations):
    hours, _, _, bins = receivers.shape
    count_src = sources.shape[2]
    lags = transform.shape[0]
    steps = bins // CHUNK
    return pl.pallas_call(
        cross_project_kernel,
        grid=(steps,),
        in_specs=[
            pl.BlockSpec((hours, 2, stations, CHUNK), lambda j: (0, 0, 0, j)),
            pl.BlockSpec((hours, 2, count_src, CHUNK), lambda j: (0, 0, 0, j)),
            pl.BlockSpec((lags, CHUNK), lambda j: (0, j)),
            pl.BlockSpec((lags, CHUNK), lambda j: (0, j + steps)),
        ],
        out_specs=pl.BlockSpec((lags, count_src * stations), lambda j: (0, 0)),
        out_shape=jax.ShapeDtypeStruct((lags, count_src * stations), jnp.float32),
        scratch_shapes=[
            pltpu.VMEM((hours, 2, count_src, ROWS, CHUNK), jnp.float32),
            pltpu.VMEM((count_src * stations, CHUNK), jnp.bfloat16),
            pltpu.VMEM((count_src * stations, CHUNK), jnp.bfloat16),
        ],
        compiler_params=pltpu.CompilerParams(dimension_semantics=("arbitrary",)),
    )(receivers, sources, transform, transform)


def reduce_lags(projected):
    index = lax.axis_index("tm")
    core = index % 2
    z_lo = index // 2
    lags, width = projected.shape
    blocks = projected.reshape(2, 2, lags // 4, width)
    keep = lax.dynamic_index_in_dim(blocks, core, axis=1, keepdims=False)
    send = lax.dynamic_index_in_dim(blocks, 1 - core, axis=1, keepdims=False)
    got = lax.ppermute(send, "tm", perm=[(0, 1), (1, 0), (2, 3), (3, 2)])
    half = keep + got
    keep = lax.dynamic_index_in_dim(half, z_lo, axis=0, keepdims=False)
    send = lax.dynamic_index_in_dim(half, 1 - z_lo, axis=0, keepdims=False)
    got = lax.ppermute(send, "tm", perm=[(0, 2), (2, 0), (1, 3), (3, 1)])
    return keep + got


def whiten(joined):
    values = joined.astype(jnp.float32)
    magnitude = jnp.sqrt(values[:, 0] * values[:, 0] + values[:, 1] * values[:, 1])
    block_num = BINS // BLOCK
    indicator = (
        lax.broadcasted_iota(jnp.int32, (BINS, block_num), 0) // BLOCK
        == lax.broadcasted_iota(jnp.int32, (BINS, block_num), 1)
    ).astype(jnp.float32)
    totals = jnp.einsum(
        "hrf,fb->hrb", magnitude, indicator, precision=lax.Precision.HIGHEST
    )
    padded = jnp.pad(totals, ((0, 0), (0, 0), (1, 1)))
    level_mean = (padded[..., :-2] + padded[..., 1:-1] + padded[..., 2:]) / (3.0 * BLOCK)
    denom = jnp.einsum(
        "hrb,fb->hrf", level_mean + EPSILON, indicator, precision=lax.Precision.HIGHEST
    )
    return (values / denom[:, None]).astype(jnp.bfloat16)


def to_send(spectra, first, count, extra):
    hours_dev, stations, _, bins_dev = spectra.shape
    shards = lax.axis_size("sta")
    chunks = spectra.reshape(hours_dev, shards, stations // shards, 2, bins_dev)
    chunks = jnp.transpose(chunks[:, :, first:first + count], (0, 3, 1, 2, 4))
    if extra is not None:
        copies = jnp.broadcast_to(
            extra[:, :, None], (hours_dev, 2, shards, extra.shape[2], bins_dev)
        )
        chunks = jnp.concatenate([chunks, copies], axis=3)
    return chunks.reshape(hours_dev, 2, -1, bins_dev)


def local(spectra, src_ids):
    hours_dev, stations, _, _ = spectra.shape
    shards = lax.axis_size("sta")
    stations_dev = stations // shards
    half = stations_dev // 2
    flat_ids = src_ids.reshape(-1)
    count_all = flat_ids.shape[0]
    src_raw = jnp.transpose(jnp.take(spectra, flat_ids, axis=1), (0, 2, 1, 3))
    send_a = to_send(spectra, 0, half, src_raw)
    joined_a = lax.all_to_all(send_a, "sta", split_axis=2, concat_axis=3, tiled=True)
    transform = make_table(hours_dev * lax.axis_size("tm"))
    spectra_b, transform = lax.optimization_barrier((spectra, transform))
    send_b = to_send(spectra_b, half, stations_dev - half, None)
    send_b, joined_a = lax.optimization_barrier((send_b, joined_a))
    joined_b = lax.all_to_all(send_b, "sta", split_axis=2, concat_axis=3, tiled=True)
    white_a = whiten(joined_a)
    row_count = transform.shape[0] // lax.axis_size("tm")
    sources = white_a[:, :, half:half + count_all]
    out_a = cross_project(white_a, sources, transform, half)
    part_a = reduce_lags(out_a)
    white_b = whiten(joined_b)
    split = (ROUNDS - 1) * NSRC
    out_b1 = cross_project(white_b, sources[:, :, :split], transform, half)
    white_b, out_b1 = lax.optimization_barrier((white_b, out_b1))
    part_b1 = reduce_lags(out_b1)
    out_b2 = cross_project(white_b, sources[:, :, split:], transform, half)
    part_b2 = reduce_lags(out_b2)
    part_b = jnp.concatenate(
        [
            part_b1.reshape(row_count, ROUNDS - 1, NSRC, half),
            part_b2.reshape(row_count, 1, NSRC, half),
        ],
        axis=1,
    )
    both = jnp.concatenate(
        [part_a.reshape(row_count, ROUNDS, NSRC, half), part_b], axis=3
    )
    return jnp.transpose(both, (1, 0, 2, 3))


def solution(mesh):
    return jax.shard_map(
        local,
        mesh=mesh,
        in_specs=(P("tm", None, None, "sta"), P()),
        out_specs=P(None, "tm", None, "sta"),
        check_vma=False,
    )
```

```python
import math

import jax
import jax.numpy as jnp
from jax import lax
from jax.experimental import pallas as pl
from jax.experimental.pallas import tpu as pltpu
from jax.sharding import PartitionSpec as P


BINS = 4096
BLOCK = 64
LAGS = 256
NSRC = 8
ROUNDS = 3

CHUNK = 512
ROWS = 16

EPSILON = 1e-05


def make_table(total_hours):
    lag_index = lax.iota(jnp.int32, LAGS) - LAGS // 2
    freq_index = lax.iota(jnp.int32, BINS)
    phase_int = jnp.remainder(lag_index[:, None] * freq_index[None, :], 2 * BINS)
    angle_rad = 2.0 * math.pi / (2 * BINS) * phase_int.astype(jnp.float32)
    norm_scale = 1.0 / math.sqrt(BINS * total_hours)
    return jnp.concatenate(
        [jnp.cos(angle_rad) * norm_scale, -jnp.sin(angle_rad) * norm_scale], axis=1
    ).astype(jnp.bfloat16)


def cross_project_kernel(x_ref, y_ref, tre_ref, tim_ref, out_ref, yb_ref, cre_ref, cim_ref):
    step = pl.program_id(0)
    hours = x_ref.shape[0]
    stations = x_ref.shape[2]
    count_src = y_ref.shape[2]
    width = x_ref.shape[3]

    @pl.when(step == 0)
    def _():
        out_ref[...] = jnp.zeros_like(out_ref)

    for h in range(hours):
        for p in range(2):
            for k in range(count_src):
                row = y_ref[h, p, pl.ds(k, 1), :].astype(jnp.float32)
                yb_ref[h, p, k] = jnp.broadcast_to(row, (ROWS, width))

    def body(r, carry):
        first = pl.multiple_of(r * ROWS, ROWS)
        xs = [
            [x_ref[h, p, pl.ds(first, ROWS), :].astype(jnp.float32) for p in range(2)]
            for h in range(hours)
        ]
        for k in range(count_src):
            real = None
            imag = None
            for h in range(hours):
                y0 = yb_ref[h, 0, k]
                y1 = yb_ref[h, 1, k]
                x0, x1 = xs[h]
                re_h = y0 * x0 + y1 * x1
                im_h = y1 * x0 - y0 * x1
                real = re_h if real is None else real + re_h
                imag = im_h if imag is None else imag + im_h
            dest = pl.ds(k * stations + first, ROWS)
            cre_ref[dest, :] = real.astype(jnp.bfloat16)
            cim_ref[dest, :] = imag.astype(jnp.bfloat16)
        return carry

    lax.fori_loop(0, stations // ROWS, body, 0)
    dims = (((1,), (1,)), ((), ()))
    span = NSRC * stations
    for rnd in range(count_src // NSRC):
        cols = pl.ds(rnd * span, span)
        out_ref[:, cols] += lax.dot_general(
            tre_ref[...], cre_ref[cols, :], dims, preferred_element_type=jnp.float32
        ) + lax.dot_general(tim_ref[...], cim_ref[cols, :], dims, preferred_element_type=jnp.float32)


def cross_project(receivers, sources, transform, stations):
    hours, _, _, bins = receivers.shape
    count_src = sources.shape[2]
    lags = transform.shape[0]
    steps = bins // CHUNK
    return pl.pallas_call(
        cross_project_kernel,
        grid=(steps,),
        in_specs=[
            pl.BlockSpec((hours, 2, stations, CHUNK), lambda j: (0, 0, 0, j)),
            pl.BlockSpec((hours, 2, count_src, CHUNK), lambda j: (0, 0, 0, j)),
            pl.BlockSpec((lags, CHUNK), lambda j: (0, j)),
            pl.BlockSpec((lags, CHUNK), lambda j: (0, j + steps)),
        ],
        out_specs=pl.BlockSpec((lags, count_src * stations), lambda j: (0, 0)),
        out_shape=jax.ShapeDtypeStruct((lags, count_src * stations), jnp.float32),
        scratch_shapes=[
            pltpu.VMEM((hours, 2, count_src, ROWS, CHUNK), jnp.float32),
            pltpu.VMEM((count_src * stations, CHUNK), jnp.bfloat16),
            pltpu.VMEM((count_src * stations, CHUNK), jnp.bfloat16),
        ],
        compiler_params=pltpu.CompilerParams(dimension_semantics=("arbitrary",)),
    )(receivers, sources, transform, transform)


def reduce_lags(projected):
    index = lax.axis_index("tm")
    core = index % 2
    z_lo = index // 2
    lags, width = projected.shape
    blocks = projected.reshape(2, 2, lags // 4, width)
    keep = lax.dynamic_index_in_dim(blocks, core, axis=1, keepdims=False)
    send = lax.dynamic_index_in_dim(blocks, 1 - core, axis=1, keepdims=False)
    got = lax.ppermute(send, "tm", perm=[(0, 1), (1, 0), (2, 3), (3, 2)])
    half = keep + got
    keep = lax.dynamic_index_in_dim(half, z_lo, axis=0, keepdims=False)
    send = lax.dynamic_index_in_dim(half, 1 - z_lo, axis=0, keepdims=False)
    got = lax.ppermute(send, "tm", perm=[(0, 2), (2, 0), (1, 3), (3, 1)])
    return keep + got


def whiten(joined):
    values = joined.astype(jnp.float32)
    magnitude = jnp.sqrt(values[:, 0] * values[:, 0] + values[:, 1] * values[:, 1])
    block_num = BINS // BLOCK
    indicator = (
        lax.broadcasted_iota(jnp.int32, (BINS, block_num), 0) // BLOCK
        == lax.broadcasted_iota(jnp.int32, (BINS, block_num), 1)
    ).astype(jnp.float32)
    totals = jnp.einsum(
        "hrf,fb->hrb", magnitude, indicator, precision=lax.Precision.HIGHEST
    )
    padded = jnp.pad(totals, ((0, 0), (0, 0), (1, 1)))
    level_mean = (padded[..., :-2] + padded[..., 1:-1] + padded[..., 2:]) / (3.0 * BLOCK)
    denom = jnp.einsum(
        "hrb,fb->hrf", level_mean + EPSILON, indicator, precision=lax.Precision.HIGHEST
    )
    return (values / denom[:, None]).astype(jnp.bfloat16)


def to_send(spectra, first, count, extra):
    hours_dev, stations, _, bins_dev = spectra.shape
    shards = lax.axis_size("sta")
    chunks = spectra.reshape(hours_dev, shards, stations // shards, 2, bins_dev)
    chunks = jnp.transpose(chunks[:, :, first:first + count], (0, 3, 1, 2, 4))
    if extra is not None:
        copies = jnp.broadcast_to(
            extra[:, :, None], (hours_dev, 2, shards, extra.shape[2], bins_dev)
        )
        chunks = jnp.concatenate([chunks, copies], axis=3)
    return chunks.reshape(hours_dev, 2, -1, bins_dev)


def local(spectra, src_ids):
    hours_dev, stations, _, _ = spectra.shape
    shards = lax.axis_size("sta")
    stations_dev = stations // shards
    half = stations_dev // 2
    flat_ids = src_ids.reshape(-1)
    count_all = flat_ids.shape[0]
    src_raw = jnp.transpose(jnp.take(spectra, flat_ids, axis=1), (0, 2, 1, 3))
    send_a = to_send(spectra, 0, half, src_raw)
    joined_a = lax.all_to_all(send_a, "sta", split_axis=2, concat_axis=3, tiled=True)
    transform = make_table(hours_dev * lax.axis_size("tm"))
    spectra_b, transform = lax.optimization_barrier((spectra, transform))
    send_b = to_send(spectra_b, half, stations_dev - half, None)
    send_b, joined_a = lax.optimization_barrier((send_b, joined_a))
    joined_b = lax.all_to_all(send_b, "sta", split_axis=2, concat_axis=3, tiled=True)
    white_a = whiten(joined_a)
    row_count = transform.shape[0] // lax.axis_size("tm")
    sources = white_a[:, :, half:half + count_all]
    out_a = cross_project(white_a, sources, transform, half)
    part_a = reduce_lags(out_a)
    white_b = whiten(joined_b)
    out_b = cross_project(white_b, sources, transform, half)
    cols = out_b.shape[1] // 2
    part_b = jnp.concatenate(
        [reduce_lags(out_b[:, :cols]), reduce_lags(out_b[:, cols:])], axis=1
    ).reshape(row_count, ROUNDS, NSRC, half)
    both = jnp.concatenate(
        [part_a.reshape(row_count, ROUNDS, NSRC, half), part_b], axis=3
    )
    return jnp.transpose(both, (1, 0, 2, 3))


def solution(mesh):
    return jax.shard_map(
        local,
        mesh=mesh,
        in_specs=(P("tm", None, None, "sta"), P()),
        out_specs=P(None, "tm", None, "sta"),
        check_vma=False,
    )
```

```python
import math

import jax
import jax.numpy as jnp
from jax import lax
from jax.experimental import pallas as pl
from jax.experimental.pallas import tpu as pltpu
from jax.sharding import PartitionSpec as P


BINS = 4096
BLOCK = 64
LAGS = 256
NSRC = 8
ROUNDS = 3

CHUNK = 512
ROWS = 16

EPSILON = 1e-05


def make_table(total_hours):
    lag_index = lax.iota(jnp.int32, LAGS) - LAGS // 2
    freq_index = lax.iota(jnp.int32, BINS)
    phase_int = jnp.remainder(lag_index[:, None] * freq_index[None, :], 2 * BINS)
    angle_rad = 2.0 * math.pi / (2 * BINS) * phase_int.astype(jnp.float32)
    norm_scale = 1.0 / math.sqrt(BINS * total_hours)
    return jnp.concatenate(
        [jnp.cos(angle_rad) * norm_scale, -jnp.sin(angle_rad) * norm_scale], axis=1
    ).astype(jnp.bfloat16)


def cross_project_kernel(x_ref, y_ref, tre_ref, tim_ref, out_ref, yb_ref, cre_ref, cim_ref):
    step = pl.program_id(0)
    hours = x_ref.shape[0]
    stations = x_ref.shape[2]
    count_src = y_ref.shape[2]
    width = x_ref.shape[3]

    @pl.when(step == 0)
    def _():
        out_ref[...] = jnp.zeros_like(out_ref)

    for h in range(hours):
        for p in range(2):
            for k in range(count_src):
                row = y_ref[h, p, pl.ds(k, 1), :].astype(jnp.float32)
                yb_ref[h, p, k] = jnp.broadcast_to(row, (ROWS, width))

    def body(r, carry):
        first = pl.multiple_of(r * ROWS, ROWS)
        xs = [
            [x_ref[h, p, pl.ds(first, ROWS), :].astype(jnp.float32) for p in range(2)]
            for h in range(hours)
        ]
        for k in range(count_src):
            real = None
            imag = None
            for h in range(hours):
                y0 = yb_ref[h, 0, k]
                y1 = yb_ref[h, 1, k]
                x0, x1 = xs[h]
                re_h = y0 * x0 + y1 * x1
                im_h = y1 * x0 - y0 * x1
                real = re_h if real is None else real + re_h
                imag = im_h if imag is None else imag + im_h
            dest = pl.ds(k * stations + first, ROWS)
            cre_ref[dest, :] = real.astype(jnp.bfloat16)
            cim_ref[dest, :] = imag.astype(jnp.bfloat16)
        return carry

    lax.fori_loop(0, stations // ROWS, body, 0)
    dims = (((1,), (1,)), ((), ()))
    span = NSRC * stations
    for rnd in range(count_src // NSRC):
        cols = pl.ds(rnd * span, span)
        out_ref[:, cols] += lax.dot_general(
            tre_ref[...], cre_ref[cols, :], dims, preferred_element_type=jnp.float32
        ) + lax.dot_general(tim_ref[...], cim_ref[cols, :], dims, preferred_element_type=jnp.float32)


def cross_project(receivers, sources, transform, stations):
    hours, _, _, bins = receivers.shape
    count_src = sources.shape[2]
    lags = transform.shape[0]
    steps = bins // CHUNK
    return pl.pallas_call(
        cross_project_kernel,
        grid=(steps,),
        in_specs=[
            pl.BlockSpec((hours, 2, stations, CHUNK), lambda j: (0, 0, 0, j)),
            pl.BlockSpec((hours, 2, count_src, CHUNK), lambda j: (0, 0, 0, j)),
            pl.BlockSpec((lags, CHUNK), lambda j: (0, j)),
            pl.BlockSpec((lags, CHUNK), lambda j: (0, j + steps)),
        ],
        out_specs=pl.BlockSpec((lags, count_src * stations), lambda j: (0, 0)),
        out_shape=jax.ShapeDtypeStruct((lags, count_src * stations), jnp.float32),
        scratch_shapes=[
            pltpu.VMEM((hours, 2, count_src, ROWS, CHUNK), jnp.float32),
            pltpu.VMEM((count_src * stations, CHUNK), jnp.bfloat16),
            pltpu.VMEM((count_src * stations, CHUNK), jnp.bfloat16),
        ],
        compiler_params=pltpu.CompilerParams(dimension_semantics=("arbitrary",)),
    )(receivers, sources, transform, transform)


def reduce_lags(projected):
    index = lax.axis_index("tm")
    core = index % 2
    z_lo = index // 2
    lags, width = projected.shape
    blocks = projected.reshape(2, 2, lags // 4, width)
    keep = lax.dynamic_index_in_dim(blocks, core, axis=1, keepdims=False)
    send = lax.dynamic_index_in_dim(blocks, 1 - core, axis=1, keepdims=False)
    got = lax.ppermute(send, "tm", perm=[(0, 1), (1, 0), (2, 3), (3, 2)])
    half = keep + got
    keep = lax.dynamic_index_in_dim(half, z_lo, axis=0, keepdims=False)
    send = lax.dynamic_index_in_dim(half, 1 - z_lo, axis=0, keepdims=False)
    got = lax.ppermute(send, "tm", perm=[(0, 2), (2, 0), (1, 3), (3, 1)])
    return keep + got


def whiten(joined):
    values = joined.astype(jnp.float32)
    magnitude = jnp.sqrt(values[:, 0] * values[:, 0] + values[:, 1] * values[:, 1])
    block_num = BINS // BLOCK
    indicator = (
        lax.broadcasted_iota(jnp.int32, (BINS, block_num), 0) // BLOCK
        == lax.broadcasted_iota(jnp.int32, (BINS, block_num), 1)
    ).astype(jnp.float32)
    totals = jnp.einsum(
        "hrf,fb->hrb", magnitude, indicator, precision=lax.Precision.HIGHEST
    )
    padded = jnp.pad(totals, ((0, 0), (0, 0), (1, 1)))
    level_mean = (padded[..., :-2] + padded[..., 1:-1] + padded[..., 2:]) / (3.0 * BLOCK)
    denom = jnp.einsum(
        "hrb,fb->hrf", level_mean + EPSILON, indicator, precision=lax.Precision.HIGHEST
    )
    return (values / denom[:, None]).astype(jnp.bfloat16)


def to_send(spectra, first, count, extra):
    hours_dev, stations, _, bins_dev = spectra.shape
    shards = lax.axis_size("sta")
    chunks = spectra.reshape(hours_dev, shards, stations // shards, 2, bins_dev)
    chunks = jnp.transpose(chunks[:, :, first:first + count], (0, 3, 1, 2, 4))
    if extra is not None:
        copies = jnp.broadcast_to(
            extra[:, :, None], (hours_dev, 2, shards, extra.shape[2], bins_dev)
        )
        chunks = jnp.concatenate([chunks, copies], axis=3)
    return chunks.reshape(hours_dev, 2, -1, bins_dev)


def reduce_direct(projected):
    index = lax.axis_index("tm")
    lags, width = projected.shape
    parts = lax.axis_size("tm")
    blocks = projected.reshape(parts, lags // parts, width)
    total = lax.dynamic_index_in_dim(blocks, index, axis=0, keepdims=False)
    for mask in range(1, parts):
        send = lax.dynamic_index_in_dim(blocks, index ^ mask, axis=0, keepdims=False)
        total = total + lax.ppermute(
            send, "tm", perm=[(i, i ^ mask) for i in range(parts)]
        )
    return total


SPLITS = (32, 48, 48)


def local(spectra, src_ids):
    hours_dev, _, _, _ = spectra.shape
    flat_ids = src_ids.reshape(-1)
    count_all = flat_ids.shape[0]
    src_raw = jnp.transpose(jnp.take(spectra, flat_ids, axis=1), (0, 2, 1, 3))
    starts = [sum(SPLITS[:i]) for i in range(len(SPLITS))]
    send = to_send(spectra, 0, SPLITS[0], src_raw)
    joined = [lax.all_to_all(send, "sta", split_axis=2, concat_axis=3, tiled=True)]
    transform = make_table(hours_dev * lax.axis_size("tm"))
    spectra_late, transform = lax.optimization_barrier((spectra, transform))
    for part in range(1, len(SPLITS)):
        send = to_send(spectra_late, starts[part], SPLITS[part], None)
        send, last = lax.optimization_barrier((send, joined[-1]))
        joined[-1] = last
        joined.append(lax.all_to_all(send, "sta", split_axis=2, concat_axis=3, tiled=True))
    row_count = transform.shape[0] // lax.axis_size("tm")
    pieces = []
    sources = None
    for part, count in enumerate(SPLITS):
        white = whiten(joined[part])
        if sources is None:
            sources = white[:, :, count:count + count_all]
        out = cross_project(white, sources, transform, count)
        if part + 1 < len(SPLITS):
            reduced = reduce_direct(out)
        else:
            cols = out.shape[1] // 2
            reduced = jnp.concatenate(
                [reduce_lags(out[:, :cols]), reduce_lags(out[:, cols:])], axis=1
            )
        pieces.append(reduced.reshape(row_count, ROUNDS, NSRC, count))
    both = jnp.concatenate(pieces, axis=3)
    return jnp.transpose(both, (1, 0, 2, 3))


def solution(mesh):
    return jax.shard_map(
        local,
        mesh=mesh,
        in_specs=(P("tm", None, None, "sta"), P()),
        out_specs=P(None, "tm", None, "sta"),
        check_vma=False,
    )
```

```python
import math

import jax
import jax.numpy as jnp
from jax import lax
from jax.experimental import pallas as pl
from jax.experimental.pallas import tpu as pltpu
from jax.sharding import PartitionSpec as P


BINS = 4096
BLOCK = 64
LAGS = 256
NSRC = 8
ROUNDS = 3

CHUNK = 1024
ROWS = 16

EPSILON = 1e-05


def make_table(total_hours):
    lag_index = lax.iota(jnp.int32, LAGS) - LAGS // 2
    freq_index = lax.iota(jnp.int32, BINS)
    phase_int = jnp.remainder(lag_index[:, None] * freq_index[None, :], 2 * BINS)
    angle_rad = 2.0 * math.pi / (2 * BINS) * phase_int.astype(jnp.float32)
    norm_scale = 1.0 / math.sqrt(BINS * total_hours)
    return jnp.concatenate(
        [jnp.cos(angle_rad) * norm_scale, -jnp.sin(angle_rad) * norm_scale], axis=1
    ).astype(jnp.bfloat16)


def cross_project_kernel(x_ref, y_ref, tre_ref, tim_ref, out_ref, yb_ref, cre_ref, cim_ref):
    step = pl.program_id(0)
    hours = x_ref.shape[0]
    stations = x_ref.shape[2]
    count_src = y_ref.shape[2]
    width = x_ref.shape[3]

    @pl.when(step == 0)
    def _():
        out_ref[...] = jnp.zeros_like(out_ref)

    for h in range(hours):
        for p in range(2):
            for k in range(count_src):
                row = y_ref[h, p, pl.ds(k, 1), :].astype(jnp.float32)
                yb_ref[h, p, k] = jnp.broadcast_to(row, (ROWS, width))

    def body(r, carry):
        first = pl.multiple_of(r * ROWS, ROWS)
        xs = [
            [x_ref[h, p, pl.ds(first, ROWS), :].astype(jnp.float32) for p in range(2)]
            for h in range(hours)
        ]
        for k in range(count_src):
            real = None
            imag = None
            for h in range(hours):
                y0 = yb_ref[h, 0, k]
                y1 = yb_ref[h, 1, k]
                x0, x1 = xs[h]
                re_h = y0 * x0 + y1 * x1
                im_h = y1 * x0 - y0 * x1
                real = re_h if real is None else real + re_h
                imag = im_h if imag is None else imag + im_h
            dest = pl.ds(k * stations + first, ROWS)
            cre_ref[dest, :] = real.astype(jnp.bfloat16)
            cim_ref[dest, :] = imag.astype(jnp.bfloat16)
        return carry

    lax.fori_loop(0, stations // ROWS, body, 0, unroll=True)
    dims = (((1,), (1,)), ((), ()))
    span = NSRC * stations
    for rnd in range(count_src // NSRC):
        cols = pl.ds(rnd * span, span)
        out_ref[:, cols] += lax.dot_general(
            tre_ref[...], cre_ref[cols, :], dims, preferred_element_type=jnp.float32
        ) + lax.dot_general(tim_ref[...], cim_ref[cols, :], dims, preferred_element_type=jnp.float32)


def cross_project(receivers, sources, transform, stations):
    hours, _, _, bins = receivers.shape
    count_src = sources.shape[2]
    lags = transform.shape[0]
    steps = bins // CHUNK
    return pl.pallas_call(
        cross_project_kernel,
        grid=(steps,),
        in_specs=[
            pl.BlockSpec((hours, 2, stations, CHUNK), lambda j: (0, 0, 0, j)),
            pl.BlockSpec((hours, 2, count_src, CHUNK), lambda j: (0, 0, 0, j)),
            pl.BlockSpec((lags, CHUNK), lambda j: (0, j)),
            pl.BlockSpec((lags, CHUNK), lambda j: (0, j + steps)),
        ],
        out_specs=pl.BlockSpec((lags, count_src * stations), lambda j: (0, 0)),
        out_shape=jax.ShapeDtypeStruct((lags, count_src * stations), jnp.float32),
        scratch_shapes=[
            pltpu.VMEM((hours, 2, count_src, ROWS, CHUNK), jnp.float32),
            pltpu.VMEM((count_src * stations, CHUNK), jnp.bfloat16),
            pltpu.VMEM((count_src * stations, CHUNK), jnp.bfloat16),
        ],
        compiler_params=pltpu.CompilerParams(dimension_semantics=("arbitrary",)),
    )(receivers, sources, transform, transform)


def reduce_lags(projected):
    index = lax.axis_index("tm")
    core = index % 2
    z_lo = index // 2
    lags, width = projected.shape
    blocks = projected.reshape(2, 2, lags // 4, width)
    keep = lax.dynamic_index_in_dim(blocks, core, axis=1, keepdims=False)
    send = lax.dynamic_index_in_dim(blocks, 1 - core, axis=1, keepdims=False)
    got = lax.ppermute(send, "tm", perm=[(0, 1), (1, 0), (2, 3), (3, 2)])
    half = keep + got
    keep = lax.dynamic_index_in_dim(half, z_lo, axis=0, keepdims=False)
    send = lax.dynamic_index_in_dim(half, 1 - z_lo, axis=0, keepdims=False)
    got = lax.ppermute(send, "tm", perm=[(0, 2), (2, 0), (1, 3), (3, 1)])
    return keep + got


def whiten(joined):
    values = joined.astype(jnp.float32)
    magnitude = jnp.sqrt(values[:, 0] * values[:, 0] + values[:, 1] * values[:, 1])
    block_num = BINS // BLOCK
    indicator = (
        lax.broadcasted_iota(jnp.int32, (BINS, block_num), 0) // BLOCK
        == lax.broadcasted_iota(jnp.int32, (BINS, block_num), 1)
    ).astype(jnp.float32)
    totals = jnp.einsum(
        "hrf,fb->hrb", magnitude, indicator, precision=lax.Precision.HIGHEST
    )
    padded = jnp.pad(totals, ((0, 0), (0, 0), (1, 1)))
    level_mean = (padded[..., :-2] + padded[..., 1:-1] + padded[..., 2:]) / (3.0 * BLOCK)
    denom = jnp.einsum(
        "hrb,fb->hrf", level_mean + EPSILON, indicator, precision=lax.Precision.HIGHEST
    )
    return (values / denom[:, None]).astype(jnp.bfloat16)


def to_send(spectra, first, count, extra):
    hours_dev, stations, _, bins_dev = spectra.shape
    shards = lax.axis_size("sta")
    chunks = spectra.reshape(hours_dev, shards, stations // shards, 2, bins_dev)
    chunks = jnp.transpose(chunks[:, :, first:first + count], (0, 3, 1, 2, 4))
    if extra is not None:
        copies = jnp.broadcast_to(
            extra[:, :, None], (hours_dev, 2, shards, extra.shape[2], bins_dev)
        )
        chunks = jnp.concatenate([chunks, copies], axis=3)
    return chunks.reshape(hours_dev, 2, -1, bins_dev)


def reduce_direct(projected):
    index = lax.axis_index("tm")
    lags, width = projected.shape
    parts = lax.axis_size("tm")
    blocks = projected.reshape(parts, lags // parts, width)
    total = lax.dynamic_index_in_dim(blocks, index, axis=0, keepdims=False)
    for mask in range(1, parts):
        send = lax.dynamic_index_in_dim(blocks, index ^ mask, axis=0, keepdims=False)
        total = total + lax.ppermute(
            send, "tm", perm=[(i, i ^ mask) for i in range(parts)]
        )
    return total


def local(spectra, src_ids):
    hours_dev, stations, _, _ = spectra.shape
    shards = lax.axis_size("sta")
    stations_dev = stations // shards
    half = stations_dev // 2
    flat_ids = src_ids.reshape(-1)
    count_all = flat_ids.shape[0]
    src_raw = jnp.transpose(jnp.take(spectra, flat_ids, axis=1), (0, 2, 1, 3))
    send_a = to_send(spectra, 0, half, src_raw)
    joined_a = lax.all_to_all(send_a, "sta", split_axis=2, concat_axis=3, tiled=True)
    transform = make_table(hours_dev * lax.axis_size("tm"))
    spectra_b, transform = lax.optimization_barrier((spectra, transform))
    send_b = to_send(spectra_b, half, stations_dev - half, None)
    send_b, joined_a = lax.optimization_barrier((send_b, joined_a))
    joined_b = lax.all_to_all(send_b, "sta", split_axis=2, concat_axis=3, tiled=True)
    white_a = whiten(joined_a)
    row_count = transform.shape[0] // lax.axis_size("tm")
    sources = white_a[:, :, half:half + count_all]
    out_a = cross_project(white_a, sources, transform, half)
    part_a = reduce_direct(out_a)
    white_b = whiten(joined_b)
    out_b = cross_project(white_b, sources, transform, half)
    cols = out_b.shape[1] // 2
    part_b = jnp.concatenate(
        [reduce_lags(out_b[:, :cols]), reduce_lags(out_b[:, cols:])], axis=1
    ).reshape(row_count, ROUNDS, NSRC, half)
    both = jnp.concatenate(
        [part_a.reshape(row_count, ROUNDS, NSRC, half), part_b], axis=3
    )
    return jnp.transpose(both, (1, 0, 2, 3))


def solution(mesh):
    return jax.shard_map(
        local,
        mesh=mesh,
        in_specs=(P("tm", None, None, "sta"), P()),
        out_specs=P(None, "tm", None, "sta"),
        check_vma=False,
    )
```
